256 devices in a mesh: cache: 8 (over y, core), dev: 32 (over x, z).
Axes of the slice: x: 4, y: 4, z: 8, core: 2. Of those that a mesh axis runs over, the one named last changes fastest.
Arguments:
- queries: bfloat16 [8, 1024, 8192], P('cache', None, 'dev'), may hold values from -8 to 8
- store_kv: bfloat16 [256, 512, 2048], P('cache', 'dev'), may hold values from -4 to 4
- self_kv: bfloat16 [8, 1024, 2048], P('cache'), may hold values from -5 to 5
- rec_states: bfloat16 [8, 512, 8192], P('cache', None, 'dev'), may hold values from -400 to 400
- norm_gain: bfloat16 [8192], P('dev'), may hold values from 0.099609375 to 1.8984375
- w_kv: bfloat16 [8192, 2048], P('dev'), may hold values from -0.0625 to 0.0625
- retrieval: int32 [8, 16], replicated, may hold values from 0 to 255, as said below
- doc_home: int32 [256], replicated, may hold values from 0 to 255, as said below
- rec_index: int32 [8, 16, 32], P('cache'), may hold values from 0 to 511, as said below
Outputs:
- attended: bfloat16 [8, 1024, 8192], P('cache', None, 'dev')
The draws below stay inside these ranges and needn't reach their ends.
Inputs may be any that keep to these rules, and one draw needn't show every extreme that they name: `retrieval`: each request names 16 distinct documents; their store rows lie in exactly 4 of the groups of 32 consecutive rows, 4 in each. `doc_home`: every store row holds exactly one document. `rec_index`: the 32 positions of one block are distinct.
All inputs are finite; a program needn't handle non-finite values.
Results may differ from the reference program's by a relative error of at most 0.0045.
Values may be sent and summed in bfloat16 or wider, within the bound.
No kernel may reach another device: no remote copies, remote signals or barrier semaphores. Data moves between devices by JAX's collectives and lax.ppermute only.
A program may use at most 128 MiB of HBM per device.

```python
import math
import jax
import jax.numpy as jnp
from jax import lax

D = 8192
QH = 64
KVH = 8
HD = 128
BLK = 512
RET = 16
CAP = 4
REC = 32
QLEN = 1024
DOC_GRP = 32
REQ = 8
DOCS = 256


def draw_queries(key, part):
    shape = (REQ, QLEN, QH * HD)
    base = 2.5 * jnp.clip(jax.random.normal(jax.random.fold_in(key, 1), shape, jnp.float32), -3.2, 3.2)
    return base.astype(jnp.bfloat16)


def draw_store_kv(key, part):
    shape = (DOCS, BLK, 2 * KVH * HD)
    base = jnp.clip(jax.random.normal(jax.random.fold_in(key, 2), shape, jnp.float32), -4.0, 4.0)
    return base.astype(jnp.bfloat16)


def draw_rec_states(key, part):
    shape = (REQ, RET * REC, D)
    row_scale = 10.0 ** jax.random.uniform(jax.random.fold_in(key, 3), (REQ, RET * REC, 1), jnp.float32)
    columns = jnp.arange(D).astype(jnp.float32) / D
    col_scale = 10.0 ** (0.25 * columns + 0.75 * jax.random.uniform(jax.random.fold_in(key, 4), (D,), jnp.float32))
    base = jnp.clip(jax.random.normal(jax.random.fold_in(key, 6), shape, jnp.float32), -4.0, 4.0)
    return (base * row_scale * col_scale[None, None, :]).astype(jnp.bfloat16)


def placement_tables(key):
    anchor = jax.random.fold_in(key, 11)
    home = jax.random.permutation(jax.random.fold_in(anchor, 1), DOCS).astype(jnp.int32)
    resident = jnp.zeros((DOCS,), jnp.int32).at[home].set(jnp.arange(DOCS, dtype=jnp.int32))
    offsets = jnp.arange(REQ, dtype=jnp.int32)

    def one_request(which):
        request_key = jax.random.fold_in(anchor, 100 + which)
        priority = jax.random.permutation(jax.random.fold_in(request_key, 1), REQ).astype(jnp.int32)
        priority = jnp.where(offsets == REQ - 1, -2, jnp.where(offsets == REQ // 2, -1, priority))
        order = jnp.argsort(priority, stable=True).astype(jnp.int32)
        used_groups = (which + order[:RET // CAP]) % REQ

        def within_group(group_slot):
            return jax.random.permutation(jax.random.fold_in(request_key, 2 + group_slot), DOC_GRP)[:CAP]
        within = jax.vmap(within_group)(jnp.arange(RET // CAP))
        store_rows = (used_groups[:, None] * DOC_GRP + within).reshape(RET)
        shuffled = jax.random.permutation(jax.random.fold_in(request_key, 999), RET)
        return resident[store_rows[shuffled]]
    chosen = jax.vmap(one_request)(jnp.arange(REQ, dtype=jnp.int32))
    return (home, chosen.astype(jnp.int32))


def draw_retrieval(key, part):
    return placement_tables(key)[1]


def draw_doc_home(key, part):
    return placement_tables(key)[0]


def draw_rec_index(key, part):

    def one_block(which):
        return jax.random.permutation(jax.random.fold_in(key, 50 + which), BLK)[:REC]
    return jax.vmap(one_block)(jnp.arange(REQ * RET)).reshape(REQ, RET, REC).astype(jnp.int32)


def block_scale(stream_key, extent, split, smallest, high):
    def one(axis_at, shards_of):
        heights = jax.random.uniform(jax.random.fold_in(jax.random.fold_in(stream_key, 6), axis_at), (shards_of,), jnp.float32, smallest / len(split), high / len(split))
        return jnp.repeat(jnp.exp(heights), extent[axis_at] // shards_of).reshape((-1,) + (1,) * (len(extent) - axis_at - 1))

    level = one(*split[0])
    for cut in split[1:]:
        level = level * one(*cut)
    return level


def centred(own_key, extent, spread, reach, shards=(), kind=jnp.bfloat16):
    entries = jax.random.normal(own_key, extent, jnp.float32) * spread
    if len(shards) > 0:
        entries = block_scale(own_key, extent, shards, -0.22, 0.18) * entries
    return jnp.clip(entries, min=-reach, max=reach).astype(kind)


def setup_inputs(seed: int = 0) -> dict:
    keys = jax.random.split(jax.random.key(seed), 10)
    return {
        "queries": draw_queries(jax.random.fold_in(keys[9], 71), 0),
        "store_kv": draw_store_kv(jax.random.fold_in(keys[9], 71), 0),
        "self_kv": centred(keys[2], (REQ, QLEN, 2 * KVH * HD), 1.0, 5.0, ((0, 8),)),
        "rec_states": draw_rec_states(jax.random.fold_in(keys[9], 71), 0),
        "norm_gain": jnp.clip(1.0 + 0.18 * jax.random.normal(keys[4], (D,), jnp.float32), 0.099609375, 1.8984375).astype(jnp.bfloat16),
        "w_kv": centred(keys[5], (D, 2 * KVH * HD), D ** -0.5, 0.0625, ((0, 32),)),
        "retrieval": draw_retrieval(jax.random.fold_in(keys[9], 71), 0),
        "doc_home": draw_doc_home(jax.random.fold_in(keys[9], 71), 0),
        "rec_index": draw_rec_index(jax.random.fold_in(keys[9], 71), 0),
    }


eps_norm = 1e-05

def head_columns(matrix, first_col):
    return lax.dynamic_slice_in_dim(matrix, first_col, HD, 1)

def reference(queries, store_kv, self_kv, rec_states, norm_gain, w_kv, retrieval, doc_home, rec_index):
    kv_width = KVH * HD
    ratio_heads = QH // KVH
    inv_root = 1.0 / math.sqrt(HD)
    visible = jnp.arange(QLEN, dtype=jnp.int32)[None, :] <= jnp.arange(QLEN, dtype=jnp.int32)[:, None]

    def one_request(request):
        wanted = lax.dynamic_index_in_dim(retrieval, request, 0, keepdims=False)
        stored_rows = jnp.take(doc_home, wanted, axis=0)
        fetched = jnp.take(store_kv, stored_rows, axis=0)
        states = lax.dynamic_index_in_dim(rec_states, request, 0, keepdims=False).astype(jnp.float32)
        mean_sq = lax.optimization_barrier(jnp.sum(states * states, axis=1)) / D
        normed = (states * norm_gain.astype(jnp.float32)[None, :] * lax.rsqrt(mean_sq + eps_norm)[:, None]).astype(jnp.bfloat16)
        redone = jnp.dot(normed, w_kv, preferred_element_type=jnp.float32).astype(jnp.bfloat16)
        redone = redone.reshape(RET, REC, 2 * kv_width)
        positions = lax.dynamic_index_in_dim(rec_index, request, 0, keepdims=False)
        onehot = positions[:, :, None] == jnp.arange(BLK, dtype=jnp.int32)[None, None, :]
        placed = jnp.einsum('kib,kic->kbc', onehot.astype(jnp.float32), redone.astype(jnp.float32), precision=lax.Precision.HIGHEST).astype(jnp.bfloat16)
        blocks = jnp.where(jnp.any(onehot, axis=1)[:, :, None], placed, fetched)
        flat_blocks = blocks.reshape(RET * BLK, 2 * kv_width)
        own_self = lax.dynamic_index_in_dim(self_kv, request, 0, keepdims=False)
        own_queries = lax.dynamic_index_in_dim(queries, request, 0, keepdims=False)

        def one_head(head_at):
            kv_head = head_at // ratio_heads
            query_rows = head_columns(own_queries, head_at * HD)
            doc_keys = head_columns(flat_blocks, kv_head * HD)
            doc_values = head_columns(flat_blocks, (KVH + kv_head) * HD)
            self_keys = head_columns(own_self, kv_head * HD)
            self_values = head_columns(own_self, (KVH + kv_head) * HD)
            doc_scores = jnp.dot(query_rows, doc_keys.T, preferred_element_type=jnp.float32) * inv_root
            self_scores = jnp.dot(query_rows, self_keys.T, preferred_element_type=jnp.float32) * inv_root
            self_scores = jnp.where(visible, self_scores, -jnp.inf)
            top = jnp.maximum(lax.optimization_barrier(jnp.max(doc_scores, axis=1)), lax.optimization_barrier(jnp.max(self_scores, axis=1)))
            doc_expd = jnp.exp(doc_scores - top[:, None])
            self_expd = jnp.exp(self_scores - top[:, None])
            total = lax.optimization_barrier(jnp.sum(doc_expd, axis=1)) + lax.optimization_barrier(jnp.sum(self_expd, axis=1))
            weighted = jnp.dot(doc_expd.astype(jnp.bfloat16), doc_values, preferred_element_type=jnp.float32)
            weighted = weighted + jnp.dot(self_expd.astype(jnp.bfloat16), self_values, preferred_element_type=jnp.float32)
            return (weighted / total[:, None]).astype(jnp.bfloat16)
        per_head = lax.map(one_head, jnp.arange(QH, dtype=jnp.int32))
        return jnp.transpose(per_head, (1, 0, 2)).reshape(QLEN, QH * HD)
    return lax.map(one_request, jnp.arange(REQ, dtype=jnp.int32))
```

```python
import math

import jax
import jax.numpy as jnp
from jax import lax
from jax.sharding import Mesh, PartitionSpec as P

D = 8192
QH = 64
KVH = 8
HD = 128
RET = 16
CAP = 4
REC = 32
DOC_GRP = 32
MODE = 1


eps_norm = 1e-05
tile_rows = 512


def own_head(wide_rows, head_count, head_size, chosen):
    shaped = wide_rows.reshape(wide_rows.shape[:-1] + (2, head_count, head_size))
    taken = lax.dynamic_index_in_dim(shaped, chosen, shaped.ndim - 2, keepdims=False)
    return taken.reshape(wide_rows.shape[:-1] + (2 * head_size,))


def pick_heads(wide_rows, head_count, head_size, chosen):
    shaped = wide_rows.reshape(wide_rows.shape[:-1] + (2, head_count, head_size))
    taken = jnp.take(shaped, chosen, axis=shaped.ndim - 2)
    moved = jnp.moveaxis(taken, shaped.ndim - 2, 0)
    return moved.reshape(moved.shape[:-2] + (2 * head_size,))


def shards(queries, store_kv, self_kv, rec_states, norm_gain, w_kv, retrieval, doc_home, rec_index):
    groups = lax.axis_size("cache")
    members = lax.axis_size("dh") * lax.axis_size("dq")
    my_group = lax.axis_index("cache")
    my_member = lax.axis_index("dh") * lax.axis_size("dq") + lax.axis_index("dq")
    per_device = QH // members
    ratio_heads = QH // KVH
    my_head = my_member * per_device // ratio_heads
    shard_rows = store_kv.shape[1]
    kv_width = store_kv.shape[2]
    inv_root = 1.0 / math.sqrt(HD)
    stored_at = jnp.take(doc_home, retrieval, axis=0)
    source = stored_at // DOC_GRP
    local_row = stored_at % DOC_GRP
    before = jnp.arange(RET)[None, :] < jnp.arange(RET)[:, None]
    same_home = source[:, :, None] == source[:, None, :]
    rank_within = jnp.sum((same_home & before[None, :, :]).astype(jnp.int32), axis=2)
    places = jnp.arange(CAP, dtype=jnp.int32)
    matching = (source[:, None, :] == my_group) & (rank_within[:, None, :] == places[None, :, None])
    pick_row = jnp.sum(jnp.where(matching, local_row[:, None, :], 0), axis=2)
    filled = jnp.any(matching, axis=2)
    outgoing = jnp.take(store_kv, pick_row.reshape(-1), axis=0).reshape(
        groups, CAP, shard_rows, kv_width
    )
    outgoing = jnp.where(filled[:, :, None, None], outgoing, jnp.zeros((), store_kv.dtype))
    my_source = lax.dynamic_index_in_dim(source, my_group, 0, keepdims=False)
    my_rank = lax.dynamic_index_in_dim(rank_within, my_group, 0, keepdims=False)
    slot_place = my_source * CAP + my_rank
    dest_heads = jnp.arange(members, dtype=jnp.int32) * per_device // ratio_heads
    arrived = lax.all_to_all(outgoing, "cache", split_axis=0, concat_axis=0, tiled=True)
    compact = jnp.take(arrived.reshape(groups * CAP, shard_rows, kv_width), slot_place, axis=0)
    spread = pick_heads(compact, KVH, HD, dest_heads)
    fetched = lax.all_to_all(spread, ("dh", "dq"), split_axis=0, concat_axis=2, tiled=True)[0]
    states = rec_states[0].astype(jnp.float32)
    rows_rec = states.shape[0]
    partial_sq = jnp.sum(states * states, axis=1)
    scaled = (states * norm_gain.astype(jnp.float32)[None, :]).astype(jnp.bfloat16)
    partial_kv = jnp.dot(scaled, w_kv, preferred_element_type=jnp.float32)
    by_head = jnp.transpose(partial_kv.reshape(rows_rec, 2, KVH, HD), (2, 0, 1, 3)).reshape(KVH, rows_rec, 2 * HD)
    sq_cols = jnp.broadcast_to(partial_sq[None, :, None], (KVH, rows_rec, HD))
    packed = jnp.concatenate([by_head, sq_cols], axis=2)
    if MODE == 0:
        summed = lax.psum(packed, ("dh", "dq"))
        summed = lax.dynamic_index_in_dim(summed, my_head, 0, keepdims=False)
    elif MODE == 1:
        head_sum = lax.psum_scatter(packed, "dh", scatter_dimension=0, tiled=True)[0]
        summed = lax.psum(head_sum, "dq")
    else:
        head_sum = lax.psum_scatter(packed, "dh", scatter_dimension=0, tiled=True)[0]
        piece = lax.psum_scatter(head_sum, "dq", scatter_dimension=0, tiled=True)
        summed = lax.all_gather(piece, "dq", axis=0, tiled=True)
    inv_rms = lax.rsqrt(summed[:, 2 * HD] / D + eps_norm)
    redone = (summed[:, : 2 * HD] * inv_rms[:, None]).astype(jnp.bfloat16)
    own_rows = redone.reshape(RET, REC, 2 * HD)
    full_block = fetched.shape[1]
    positions = rec_index[0]
    onehot = positions[:, :, None] == jnp.arange(full_block, dtype=jnp.int32)[None, None, :]
    placed = jnp.einsum(
        "kib,kic->kbc", onehot.astype(jnp.bfloat16), own_rows, preferred_element_type=jnp.float32
    ).astype(jnp.bfloat16)
    replaced_at = jnp.any(onehot, axis=1)
    blocks = jnp.where(replaced_at[:, :, None], placed, fetched)
    doc_keys = blocks[:, :, :HD].reshape(-1, HD)
    doc_values = blocks[:, :, HD:].reshape(-1, HD)
    own_self = own_head(self_kv[0], KVH, HD, my_head)
    self_keys = own_self[:, :HD]
    self_values = own_self[:, HD:]
    prompt = queries.shape[1]
    head_rows = jnp.transpose(queries[0].reshape(prompt, per_device, HD), (1, 0, 2))
    block_len = min(tile_rows, prompt)
    block_count = prompt // block_len
    key_spots = jnp.arange(prompt, dtype=jnp.int32)

    def attend(pair_index):
        head_at = pair_index // block_count
        first_row = pair_index % block_count * block_len
        query_block = lax.dynamic_slice_in_dim(
            lax.dynamic_index_in_dim(head_rows, head_at, 0, keepdims=False), first_row, block_len, 0
        )
        doc_scores = (
            jnp.einsum("qd,kd->qk", query_block, doc_keys, preferred_element_type=jnp.float32)
            * inv_root
        )
        self_scores = (
            jnp.einsum("qd,kd->qk", query_block, self_keys, preferred_element_type=jnp.float32)
            * inv_root
        )
        allowed = (
            key_spots[None, :] <= (first_row + jnp.arange(block_len, dtype=jnp.int32))[:, None]
        )
        self_scores = jnp.where(allowed, self_scores, -jnp.inf)
        top = jnp.maximum(jnp.max(doc_scores, axis=1), jnp.max(self_scores, axis=1))
        doc_expd = jnp.exp(doc_scores - top[:, None])
        self_expd = jnp.exp(self_scores - top[:, None])
        total = jnp.sum(doc_expd, axis=1) + jnp.sum(self_expd, axis=1)
        weighted = jnp.dot(
            doc_expd.astype(jnp.bfloat16), doc_values, preferred_element_type=jnp.float32
        )
        weighted = weighted + jnp.dot(
            self_expd.astype(jnp.bfloat16), self_values, preferred_element_type=jnp.float32
        )
        return (weighted / total[:, None]).astype(jnp.bfloat16)

    gathered_out = lax.map(attend, jnp.arange(per_device * block_count, dtype=jnp.int32))
    result = jnp.transpose(gathered_out.reshape(per_device, prompt, HD), (1, 0, 2))
    return result.reshape(1, prompt, per_device * HD)


def solution(mesh):
    dev = ("dh", "dq")
    groups = mesh.shape["cache"]
    members = mesh.shape["dev"]
    view = Mesh(mesh.devices.reshape(groups, KVH, members // KVH), ("cache", "dh", "dq"))
    placed = (
        P("cache", None, dev),
        P("cache", dev, None),
        P("cache", None, None),
        P("cache", None, dev),
        P(dev),
        P(dev, None),
        P(),
        P(),
        P("cache", None, None),
    )
    return jax.shard_map(
        shards, mesh=view, in_specs=placed, out_specs=P("cache", None, dev), check_vma=False
    )
```

```python
import functools
import math

import jax
import jax.numpy as jnp
from jax import lax
from jax.experimental import pallas as pl
from jax.experimental.pallas import tpu as pltpu
from jax.sharding import Mesh, PartitionSpec as P

D = 8192
QH = 64
KVH = 8
HD = 128
RET = 16
CAP = 4
REC = 32
DOC_GRP = 32
MODE = 2
SQ_ROWS = 128


eps_norm = 1e-05
tile_rows = 512


def own_head(wide_rows, head_count, head_size, chosen):
    shaped = wide_rows.reshape(wide_rows.shape[:-1] + (2, head_count, head_size))
    taken = lax.dynamic_index_in_dim(shaped, chosen, shaped.ndim - 2, keepdims=False)
    return taken.reshape(wide_rows.shape[:-1] + (2 * head_size,))


def pick_heads(wide_rows, head_count, head_size, chosen):
    shaped = wide_rows.reshape(wide_rows.shape[:-1] + (2, head_count, head_size))
    taken = jnp.take(shaped, chosen, axis=shaped.ndim - 2)
    moved = jnp.moveaxis(taken, shaped.ndim - 2, 0)
    return moved.reshape(moved.shape[:-2] + (2 * head_size,))


def attn_kernel(q_ref, kd_ref, vd_ref, ks_ref, vs_ref, o_ref, m_sc, l_sc, acc_sc, *, n_doc, n_self, blk, inv_root):
    phase = pl.program_id(1)
    j = pl.program_id(2)
    rows = q_ref.shape[0]

    @pl.when((phase == 0) & (j == 0))
    def _():
        m_sc[...] = jnp.full(m_sc.shape, -jnp.inf, jnp.float32)
        l_sc[...] = jnp.zeros(l_sc.shape, jnp.float32)
        acc_sc[...] = jnp.zeros(acc_sc.shape, jnp.float32)

    def scores(k_ref, first_key):
        s = lax.dot_general(q_ref[...], k_ref[...], (((1,), (1,)), ((), ())),
                            preferred_element_type=jnp.float32) * inv_root
        if first_key is None:
            return s
        t = lax.broadcasted_iota(jnp.int32, s.shape, 0)
        u = lax.broadcasted_iota(jnp.int32, s.shape, 1) + first_key
        return jnp.where(u <= t, s, -jnp.inf)

    def step(k_ref, v_ref, first_key):
        @pl.when(phase == 0)
        def _():
            s = scores(k_ref, first_key)
            m_sc[...] = jnp.maximum(m_sc[...], jnp.max(s, axis=1, keepdims=True))

        @pl.when(phase == 1)
        def _():
            s = scores(k_ref, first_key)
            e = jnp.exp(s - m_sc[:, :1])
            l_sc[...] = l_sc[...] + jnp.sum(e, axis=1, keepdims=True)
            acc_sc[...] = acc_sc[...] + jnp.dot(e.astype(jnp.bfloat16), v_ref[...],
                                                preferred_element_type=jnp.float32)

    @pl.when(j < n_doc)
    def _():
        step(kd_ref, vd_ref, None)

    for b in range(n_self):
        @pl.when(j == n_doc + b)
        def _(b=b):
            step(ks_ref, vs_ref, b * blk)

    @pl.when((phase == 1) & (j == pl.num_programs(2) - 1))
    def _():
        o_ref[...] = (acc_sc[...] / l_sc[:, :1]).astype(o_ref.dtype)


def attention(q2d, blocks, own_self):
    T, width = q2d.shape
    heads = width // HD
    n_doc, blk, _ = blocks.shape
    n_self = T // blk
    last_doc = n_doc - 1
    kern = functools.partial(attn_kernel, n_doc=n_doc, n_self=n_self, blk=blk, inv_root=1.0 / math.sqrt(HD))
    doc_at = lambda j: jnp.minimum(j, last_doc)
    self_at = lambda j: jnp.maximum(j - n_doc, 0)
    return pl.pallas_call(
        kern,
        grid=(heads, 2, n_doc + n_self),
        in_specs=[
            pl.BlockSpec((T, HD), lambda h, p, j: (0, h)),
            pl.BlockSpec((None, blk, HD), lambda h, p, j: (doc_at(j), 0, 0)),
            pl.BlockSpec((None, blk, HD), lambda h, p, j: (doc_at(j), 0, 1)),
            pl.BlockSpec((blk, HD), lambda h, p, j: (self_at(j), 0)),
            pl.BlockSpec((blk, HD), lambda h, p, j: (self_at(j), 1)),
        ],
        out_specs=pl.BlockSpec((T, HD), lambda h, p, j: (0, h)),
        out_shape=jax.ShapeDtypeStruct((T, width), q2d.dtype),
        scratch_shapes=[pltpu.VMEM((T, HD), jnp.float32)] * 3,
    )(q2d, blocks, blocks, own_self, own_self)


def shards(queries, store_kv, self_kv, rec_states, norm_gain, w_kv, retrieval, doc_home, rec_index):
    groups = lax.axis_size("cache")
    members = lax.axis_size("dh") * lax.axis_size("dq")
    my_group = lax.axis_index("cache")
    my_member = lax.axis_index("dh") * lax.axis_size("dq") + lax.axis_index("dq")
    per_device = QH // members
    ratio_heads = QH // KVH
    my_head = my_member * per_device // ratio_heads
    shard_rows = store_kv.shape[1]
    kv_width = store_kv.shape[2]
    inv_root = 1.0 / math.sqrt(HD)
    stored_at = jnp.take(doc_home, retrieval, axis=0)
    source = stored_at // DOC_GRP
    local_row = stored_at % DOC_GRP
    before = jnp.arange(RET)[None, :] < jnp.arange(RET)[:, None]
    same_home = source[:, :, None] == source[:, None, :]
    rank_within = jnp.sum((same_home & before[None, :, :]).astype(jnp.int32), axis=2)
    places = jnp.arange(CAP, dtype=jnp.int32)
    matching = (source[:, None, :] == my_group) & (rank_within[:, None, :] == places[None, :, None])
    pick_row = jnp.sum(jnp.where(matching, local_row[:, None, :], 0), axis=2)
    filled = jnp.any(matching, axis=2)
    outgoing = jnp.take(store_kv, pick_row.reshape(-1), axis=0).reshape(
        groups, CAP, shard_rows, kv_width
    )
    outgoing = jnp.where(filled[:, :, None, None], outgoing, jnp.zeros((), store_kv.dtype))
    my_source = lax.dynamic_index_in_dim(source, my_group, 0, keepdims=False)
    my_rank = lax.dynamic_index_in_dim(rank_within, my_group, 0, keepdims=False)
    slot_place = my_source * CAP + my_rank
    dest_heads = jnp.arange(members, dtype=jnp.int32) * per_device // ratio_heads
    arrived = lax.all_to_all(outgoing, "cache", split_axis=0, concat_axis=0, tiled=True)
    compact = jnp.take(arrived.reshape(groups * CAP, shard_rows, kv_width), slot_place, axis=0)
    spread = pick_heads(compact, KVH, HD, dest_heads)
    fetched = lax.all_to_all(spread, ("dh", "dq"), split_axis=0, concat_axis=2, tiled=True)[0]
    states = rec_states[0].astype(jnp.float32)
    rows_rec = states.shape[0]
    partial_sq = jnp.sum(states * states, axis=1)
    if MODE == 0:
        total_sq = lax.psum(partial_sq, ("dh", "dq"))
    elif MODE == 1:
        total_sq = lax.psum(lax.psum(partial_sq, "dq"), "dh")
    else:
        total_sq = lax.psum(jnp.broadcast_to(partial_sq[None, :], (SQ_ROWS, rows_rec)), ("dh", "dq"))[0]
    inv_rms = lax.rsqrt(total_sq / D + eps_norm)
    normed = (states * norm_gain.astype(jnp.float32)[None, :] * inv_rms[:, None]).astype(jnp.bfloat16)
    partial_kv = jnp.dot(normed, w_kv, preferred_element_type=jnp.float32)
    by_head = jnp.transpose(partial_kv.reshape(rows_rec, 2, KVH, HD), (2, 0, 1, 3)).reshape(KVH, rows_rec, 2 * HD)
    head_sum = lax.psum_scatter(by_head, "dh", scatter_dimension=0, tiled=True)[0]
    redone = lax.psum(head_sum, "dq")
    own_rows = redone.reshape(RET, REC, 2 * HD)
    full_block = fetched.shape[1]
    positions = rec_index[0]
    onehot = positions[:, :, None] == jnp.arange(full_block, dtype=jnp.int32)[None, None, :]
    placed = jnp.einsum(
        "kib,kic->kbc", onehot.astype(jnp.float32), own_rows, precision=lax.Precision.HIGHEST
    ).astype(jnp.bfloat16)
    replaced_at = jnp.any(onehot, axis=1)
    blocks = jnp.where(replaced_at[:, :, None], placed, fetched)
    own_self = own_head(self_kv[0], KVH, HD, my_head)
    return attention(queries[0], blocks, own_self)[None]


def solution(mesh):
    dev = ("dh", "dq")
    groups = mesh.shape["cache"]
    members = mesh.shape["dev"]
    view = Mesh(mesh.devices.reshape(groups, KVH, members // KVH), ("cache", "dh", "dq"))
    placed = (
        P("cache", None, dev),
        P("cache", dev, None),
        P("cache", None, None),
        P("cache", None, dev),
        P(dev),
        P(dev, None),
        P(),
        P(),
        P("cache", None, None),
    )
    return jax.shard_map(
        shards, mesh=view, in_specs=placed, out_specs=P("cache", None, dev), check_vma=False
    )
```

```python
import functools
import math

import jax
import jax.numpy as jnp
from jax import lax
from jax.experimental import pallas as pl
from jax.experimental.pallas import tpu as pltpu
from jax.sharding import Mesh, PartitionSpec as P

D = 8192
QH = 64
KVH = 8
HD = 128
RET = 16
CAP = 4
REC = 32
DOC_GRP = 32


eps_norm = 1e-05
tile_rows = 512


def own_head(wide_rows, head_count, head_size, chosen):
    shaped = wide_rows.reshape(wide_rows.shape[:-1] + (2, head_count, head_size))
    taken = lax.dynamic_index_in_dim(shaped, chosen, shaped.ndim - 2, keepdims=False)
    return taken.reshape(wide_rows.shape[:-1] + (2 * head_size,))


def pick_heads(wide_rows, head_count, head_size, chosen):
    shaped = wide_rows.reshape(wide_rows.shape[:-1] + (2, head_count, head_size))
    taken = jnp.take(shaped, chosen, axis=shaped.ndim - 2)
    moved = jnp.moveaxis(taken, shaped.ndim - 2, 0)
    return moved.reshape(moved.shape[:-2] + (2 * head_size,))


def attn_kernel(q_ref, kd_ref, vd_ref, ks_ref, vs_ref, o_ref, m_sc, l_sc, acc_sc, *, n_doc, n_self, blk, inv_root):
    phase = pl.program_id(1)
    j = pl.program_id(2)
    rows = q_ref.shape[0]

    @pl.when((phase == 0) & (j == 0))
    def _():
        m_sc[...] = jnp.full(m_sc.shape, -jnp.inf, jnp.float32)
        l_sc[...] = jnp.zeros(l_sc.shape, jnp.float32)
        acc_sc[...] = jnp.zeros(acc_sc.shape, jnp.float32)

    def scores(k_ref, first_key):
        s = lax.dot_general(q_ref[...], k_ref[...], (((1,), (1,)), ((), ())),
                            preferred_element_type=jnp.float32) * inv_root
        if first_key is None:
            return s
        t = lax.broadcasted_iota(jnp.int32, s.shape, 0)
        u = lax.broadcasted_iota(jnp.int32, s.shape, 1) + first_key
        return jnp.where(u <= t, s, -jnp.inf)

    def step(k_ref, v_ref, first_key):
        @pl.when(phase == 0)
        def _():
            s = scores(k_ref, first_key)
            m_sc[...] = jnp.maximum(m_sc[...], jnp.max(s, axis=1, keepdims=True))

        @pl.when(phase == 1)
        def _():
            s = scores(k_ref, first_key)
            e = jnp.exp(s - m_sc[:, :1])
            l_sc[...] = l_sc[...] + jnp.sum(e, axis=1, keepdims=True)
            acc_sc[...] = acc_sc[...] + jnp.dot(e.astype(jnp.bfloat16), v_ref[...],
                                                preferred_element_type=jnp.float32)

    @pl.when(j < n_doc)
    def _():
        step(kd_ref, vd_ref, None)

    for b in range(n_self):
        @pl.when(j == n_doc + b)
        def _(b=b):
            step(ks_ref, vs_ref, b * blk)

    @pl.when((phase == 1) & (j == pl.num_programs(2) - 1))
    def _():
        o_ref[...] = (acc_sc[...] / l_sc[:, :1]).astype(o_ref.dtype)


def attention(q2d, blocks, own_self):
    T, width = q2d.shape
    heads = width // HD
    n_doc, blk, _ = blocks.shape
    n_self = T // blk
    last_doc = n_doc - 1
    kern = functools.partial(attn_kernel, n_doc=n_doc, n_self=n_self, blk=blk, inv_root=1.0 / math.sqrt(HD))
    doc_at = lambda j: jnp.minimum(j, last_doc)
    self_at = lambda j: jnp.maximum(j - n_doc, 0)
    return pl.pallas_call(
        kern,
        grid=(heads, 2, n_doc + n_self),
        in_specs=[
            pl.BlockSpec((T, HD), lambda h, p, j: (0, h)),
            pl.BlockSpec((None, blk, HD), lambda h, p, j: (doc_at(j), 0, 0)),
            pl.BlockSpec((None, blk, HD), lambda h, p, j: (doc_at(j), 0, 1)),
            pl.BlockSpec((blk, HD), lambda h, p, j: (self_at(j), 0)),
            pl.BlockSpec((blk, HD), lambda h, p, j: (self_at(j), 1)),
        ],
        out_specs=pl.BlockSpec((T, HD), lambda h, p, j: (0, h)),
        out_shape=jax.ShapeDtypeStruct((T, width), q2d.dtype),
        scratch_shapes=[pltpu.VMEM((T, HD), jnp.float32)] * 3,
    )(q2d, blocks, blocks, own_self, own_self)


def pair_sum(value, axis):
    size = lax.axis_size(axis)
    step = 1
    while step < size:
        value = value + lax.ppermute(value, axis, [(i, i ^ step) for i in range(size)])
        step *= 2
    return value


def shards(queries, store_kv, self_kv, rec_states, norm_gain, w_kv, retrieval, doc_home, rec_index):
    groups = lax.axis_size("cache")
    members = lax.axis_size("dh") * lax.axis_size("dq")
    my_group = lax.axis_index("cache")
    my_member = lax.axis_index("dh") * lax.axis_size("dq") + lax.axis_index("dq")
    per_device = QH // members
    ratio_heads = QH // KVH
    my_head = my_member * per_device // ratio_heads
    shard_rows = store_kv.shape[1]
    kv_width = store_kv.shape[2]
    inv_root = 1.0 / math.sqrt(HD)
    stored_at = jnp.take(doc_home, retrieval, axis=0)
    source = stored_at // DOC_GRP
    local_row = stored_at % DOC_GRP
    before = jnp.arange(RET)[None, :] < jnp.arange(RET)[:, None]
    same_home = source[:, :, None] == source[:, None, :]
    rank_within = jnp.sum((same_home & before[None, :, :]).astype(jnp.int32), axis=2)
    places = jnp.arange(CAP, dtype=jnp.int32)
    matching = (source[:, None, :] == my_group) & (rank_within[:, None, :] == places[None, :, None])
    pick_row = jnp.sum(jnp.where(matching, local_row[:, None, :], 0), axis=2)
    filled = jnp.any(matching, axis=2)
    outgoing = jnp.take(store_kv, pick_row.reshape(-1), axis=0).reshape(
        groups, CAP, shard_rows, kv_width
    )
    outgoing = jnp.where(filled[:, :, None, None], outgoing, jnp.zeros((), store_kv.dtype))
    my_source = lax.dynamic_index_in_dim(source, my_group, 0, keepdims=False)
    my_rank = lax.dynamic_index_in_dim(rank_within, my_group, 0, keepdims=False)
    slot_place = my_source * CAP + my_rank
    dest_heads = jnp.arange(members, dtype=jnp.int32) * per_device // ratio_heads
    arrived = lax.all_to_all(outgoing, "cache", split_axis=0, concat_axis=0, tiled=True)
    compact = jnp.take(arrived.reshape(groups * CAP, shard_rows, kv_width), slot_place, axis=0)
    spread = pick_heads(compact, KVH, HD, dest_heads)
    fetched = lax.all_to_all(spread, ("dh", "dq"), split_axis=0, concat_axis=2, tiled=True)[0]
    states = rec_states[0].astype(jnp.float32)
    rows_rec = states.shape[0]
    partial_sq = jnp.sum(states * states, axis=1)
    total_sq = pair_sum(pair_sum(partial_sq, "dq"), "dh")
    inv_rms = lax.rsqrt(total_sq / D + eps_norm)
    normed = (states * norm_gain.astype(jnp.float32)[None, :] * inv_rms[:, None]).astype(jnp.bfloat16)
    partial_kv = jnp.dot(normed, w_kv, preferred_element_type=jnp.float32)
    by_head = jnp.transpose(partial_kv.reshape(rows_rec, 2, KVH, HD), (2, 0, 1, 3)).reshape(KVH, rows_rec, 2 * HD)
    head_parts = lax.all_to_all(by_head, "dh", split_axis=0, concat_axis=0, tiled=True)
    redone = pair_sum(jnp.sum(head_parts, axis=0), "dq")
    own_rows = redone.reshape(RET, REC, 2 * HD)
    full_block = fetched.shape[1]
    positions = rec_index[0]
    onehot = positions[:, :, None] == jnp.arange(full_block, dtype=jnp.int32)[None, None, :]
    placed = jnp.einsum(
        "kib,kic->kbc", onehot.astype(jnp.float32), own_rows, precision=lax.Precision.HIGHEST
    ).astype(jnp.bfloat16)
    replaced_at = jnp.any(onehot, axis=1)
    blocks = jnp.where(replaced_at[:, :, None], placed, fetched)
    own_self = own_head(self_kv[0], KVH, HD, my_head)
    return attention(queries[0], blocks, own_self)[None]


def solution(mesh):
    dev = ("dh", "dq")
    groups = mesh.shape["cache"]
    members = mesh.shape["dev"]
    view = Mesh(mesh.devices.reshape(groups, KVH, members // KVH), ("cache", "dh", "dq"))
    placed = (
        P("cache", None, dev),
        P("cache", dev, None),
        P("cache", None, None),
        P("cache", None, dev),
        P(dev),
        P(dev, None),
        P(),
        P(),
        P("cache", None, None),
    )
    return jax.shard_map(
        shards, mesh=view, in_specs=placed, out_specs=P("cache", None, dev), check_vma=False
    )
```

```python
import functools
import math

import jax
import jax.numpy as jnp
from jax import lax
from jax.experimental import pallas as pl
from jax.experimental.pallas import tpu as pltpu
from jax.sharding import Mesh, PartitionSpec as P

D = 8192
QH = 64
KVH = 8
HD = 128
RET = 16
CAP = 4
REC = 32
DOC_GRP = 32


eps_norm = 1e-05
tile_rows = 512


def own_head(wide_rows, head_count, head_size, chosen):
    shaped = wide_rows.reshape(wide_rows.shape[:-1] + (2, head_count, head_size))
    taken = lax.dynamic_index_in_dim(shaped, chosen, shaped.ndim - 2, keepdims=False)
    return taken.reshape(wide_rows.shape[:-1] + (2 * head_size,))


def pick_heads(wide_rows, head_count, head_size, chosen):
    shaped = wide_rows.reshape(wide_rows.shape[:-1] + (2, head_count, head_size))
    taken = jnp.take(shaped, chosen, axis=shaped.ndim - 2)
    moved = jnp.moveaxis(taken, shaped.ndim - 2, 0)
    return moved.reshape(moved.shape[:-2] + (2 * head_size,))


def attn_kernel(q_ref, kd_ref, vd_ref, ks_ref, vs_ref, o_ref, m_sc, l_sc, acc_sc, *, n_doc, n_self, blk, inv_root):
    phase = pl.program_id(1)
    j = pl.program_id(2)
    rows = q_ref.shape[0]

    @pl.when((phase == 0) & (j == 0))
    def _():
        m_sc[...] = jnp.full(m_sc.shape, -jnp.inf, jnp.float32)
        l_sc[...] = jnp.zeros(l_sc.shape, jnp.float32)
        acc_sc[...] = jnp.zeros(acc_sc.shape, jnp.float32)

    def scores(k_ref, first_key):
        s = lax.dot_general(q_ref[...], k_ref[...], (((1,), (1,)), ((), ())),
                            preferred_element_type=jnp.float32) * inv_root
        if first_key is None:
            return s
        t = lax.broadcasted_iota(jnp.int32, s.shape, 0)
        u = lax.broadcasted_iota(jnp.int32, s.shape, 1) + first_key
        return jnp.where(u <= t, s, -jnp.inf)

    def step(k_ref, v_ref, first_key):
        @pl.when(phase == 0)
        def _():
            s = scores(k_ref, first_key)
            m_sc[...] = jnp.maximum(m_sc[...], jnp.max(s, axis=1, keepdims=True))

        @pl.when(phase == 1)
        def _():
            s = scores(k_ref, first_key)
            e = jnp.exp(s - m_sc[:, :1])
            l_sc[...] = l_sc[...] + jnp.sum(e, axis=1, keepdims=True)
            acc_sc[...] = acc_sc[...] + jnp.dot(e.astype(jnp.bfloat16), v_ref[...],
                                                preferred_element_type=jnp.float32)

    @pl.when(j < n_doc)
    def _():
        step(kd_ref, vd_ref, None)

    for b in range(n_self):
        @pl.when(j == n_doc + b)
        def _(b=b):
            step(ks_ref, vs_ref, b * blk)

    @pl.when((phase == 1) & (j == pl.num_programs(2) - 1))
    def _():
        o_ref[...] = (acc_sc[...] / l_sc[:, :1]).astype(o_ref.dtype)


def attention(q2d, blocks, own_self):
    T, width = q2d.shape
    heads = width // HD
    n_doc, blk, _ = blocks.shape
    n_self = T // blk
    last_doc = n_doc - 1
    kern = functools.partial(attn_kernel, n_doc=n_doc, n_self=n_self, blk=blk, inv_root=1.0 / math.sqrt(HD))
    doc_at = lambda j: jnp.minimum(j, last_doc)
    self_at = lambda j: jnp.maximum(j - n_doc, 0)
    return pl.pallas_call(
        kern,
        grid=(heads, 2, n_doc + n_self),
        in_specs=[
            pl.BlockSpec((T, HD), lambda h, p, j: (0, h)),
            pl.BlockSpec((None, blk, HD), lambda h, p, j: (doc_at(j), 0, 0)),
            pl.BlockSpec((None, blk, HD), lambda h, p, j: (doc_at(j), 0, 1)),
            pl.BlockSpec((blk, HD), lambda h, p, j: (self_at(j), 0)),
            pl.BlockSpec((blk, HD), lambda h, p, j: (self_at(j), 1)),
        ],
        out_specs=pl.BlockSpec((T, HD), lambda h, p, j: (0, h)),
        out_shape=jax.ShapeDtypeStruct((T, width), q2d.dtype),
        scratch_shapes=[pltpu.VMEM((T, HD), jnp.float32)] * 3,
    )(q2d, blocks, blocks, own_self, own_self)


def pair_sum(value, axis):
    size = lax.axis_size(axis)
    step = 1
    while step < size:
        value = value + lax.ppermute(value, axis, [(i, i ^ step) for i in range(size)])
        step *= 2
    return value


def halve_sum(value, axis):
    size = lax.axis_size(axis)
    me = lax.axis_index(axis)
    step = 1
    while step < size:
        bit = (me // step) % 2
        halves = value.reshape((2, value.shape[0] // 2) + value.shape[1:])
        keep = lax.dynamic_index_in_dim(halves, bit, 0, keepdims=False)
        send = lax.dynamic_index_in_dim(halves, 1 - bit, 0, keepdims=False)
        value = keep + lax.ppermute(send, axis, [(i, i ^ step) for i in range(size)])
        step *= 2
    return value


def double_gather(value, axis):
    size = lax.axis_size(axis)
    me = lax.axis_index(axis)
    step = size // 2
    while step >= 1:
        bit = (me // step) % 2
        other = lax.ppermute(value, axis, [(i, i ^ step) for i in range(size)])
        value = jnp.where(
            bit == 0, jnp.concatenate([value, other], axis=0), jnp.concatenate([other, value], axis=0)
        )
        step //= 2
    return value


def shards(queries, store_kv, self_kv, rec_states, norm_gain, w_kv, retrieval, doc_home, rec_index):
    groups = lax.axis_size("cache")
    members = lax.axis_size("dh") * lax.axis_size("dq")
    my_group = lax.axis_index("cache")
    my_member = lax.axis_index("dh") * lax.axis_size("dq") + lax.axis_index("dq")
    per_device = QH // members
    ratio_heads = QH // KVH
    my_head = my_member * per_device // ratio_heads
    shard_rows = store_kv.shape[1]
    kv_width = store_kv.shape[2]
    inv_root = 1.0 / math.sqrt(HD)
    stored_at = jnp.take(doc_home, retrieval, axis=0)
    source = stored_at // DOC_GRP
    local_row = stored_at % DOC_GRP
    before = jnp.arange(RET)[None, :] < jnp.arange(RET)[:, None]
    same_home = source[:, :, None] == source[:, None, :]
    rank_within = jnp.sum((same_home & before[None, :, :]).astype(jnp.int32), axis=2)
    places = jnp.arange(CAP, dtype=jnp.int32)
    matching = (source[:, None, :] == my_group) & (rank_within[:, None, :] == places[None, :, None])
    pick_row = jnp.sum(jnp.where(matching, local_row[:, None, :], 0), axis=2)
    filled = jnp.any(matching, axis=2)
    outgoing = jnp.take(store_kv, pick_row.reshape(-1), axis=0).reshape(
        groups, CAP, shard_rows, kv_width
    )
    outgoing = jnp.where(filled[:, :, None, None], outgoing, jnp.zeros((), store_kv.dtype))
    my_source = lax.dynamic_index_in_dim(source, my_group, 0, keepdims=False)
    my_rank = lax.dynamic_index_in_dim(rank_within, my_group, 0, keepdims=False)
    slot_place = my_source * CAP + my_rank
    dest_heads = jnp.arange(members, dtype=jnp.int32) * per_device // ratio_heads
    arrived = lax.all_to_all(outgoing, "cache", split_axis=0, concat_axis=0, tiled=True)
    compact = jnp.take(arrived.reshape(groups * CAP, shard_rows, kv_width), slot_place, axis=0)
    spread = pick_heads(compact, KVH, HD, dest_heads)
    fetched = lax.all_to_all(spread, ("dh", "dq"), split_axis=0, concat_axis=2, tiled=True)[0]
    states = rec_states[0].astype(jnp.float32)
    rows_rec = states.shape[0]
    partial_sq = jnp.sum(states * states, axis=1)
    total_sq = pair_sum(pair_sum(partial_sq, "dq"), "dh")
    inv_rms = lax.rsqrt(total_sq / D + eps_norm)
    normed = (states * norm_gain.astype(jnp.float32)[None, :] * inv_rms[:, None]).astype(jnp.bfloat16)
    partial_kv = jnp.dot(normed, w_kv, preferred_element_type=jnp.float32)
    row_part = halve_sum(partial_kv, "dq")
    part_rows = row_part.shape[0]
    by_head = jnp.transpose(row_part.reshape(part_rows, 2, KVH, HD), (2, 0, 1, 3))
    head_parts = lax.all_to_all(by_head, "dh", split_axis=0, concat_axis=0, tiled=True)
    head_rows = jnp.sum(head_parts, axis=0).reshape(part_rows, 2 * HD).astype(jnp.bfloat16)
    redone = double_gather(head_rows, "dq")
    own_rows = redone.reshape(RET, REC, 2 * HD)
    full_block = fetched.shape[1]
    positions = rec_index[0]
    onehot = positions[:, :, None] == jnp.arange(full_block, dtype=jnp.int32)[None, None, :]
    placed = jnp.einsum(
        "kib,kic->kbc", onehot.astype(jnp.bfloat16), own_rows, preferred_element_type=jnp.float32
    ).astype(jnp.bfloat16)
    replaced_at = jnp.any(onehot, axis=1)
    blocks = jnp.where(replaced_at[:, :, None], placed, fetched)
    own_self = own_head(self_kv[0], KVH, HD, my_head)
    return attention(queries[0], blocks, own_self)[None]


def solution(mesh):
    dev = ("dh", "dq")
    groups = mesh.shape["cache"]
    members = mesh.shape["dev"]
    view = Mesh(mesh.devices.reshape(groups, KVH, members // KVH), ("cache", "dh", "dq"))
    placed = (
        P("cache", None, dev),
        P("cache", dev, None),
        P("cache", None, None),
        P("cache", None, dev),
        P(dev),
        P(dev, None),
        P(),
        P(),
        P("cache", None, None),
    )
    return jax.shard_map(
        shards, mesh=view, in_specs=placed, out_specs=P("cache", None, dev), check_vma=False
    )
```

```python
import functools
import math

import jax
import jax.numpy as jnp
from jax import lax
from jax.experimental import pallas as pl
from jax.experimental.pallas import tpu as pltpu
from jax.sharding import Mesh, PartitionSpec as P

D = 8192
QH = 64
KVH = 8
HD = 128
RET = 16
CAP = 4
REC = 32
DOC_GRP = 32


eps_norm = 1e-05
tile_rows = 512


def own_head(wide_rows, head_count, head_size, chosen):
    shaped = wide_rows.reshape(wide_rows.shape[:-1] + (2, head_count, head_size))
    taken = lax.dynamic_index_in_dim(shaped, chosen, shaped.ndim - 2, keepdims=False)
    return taken.reshape(wide_rows.shape[:-1] + (2 * head_size,))


def pick_heads(wide_rows, head_count, head_size, chosen):
    shaped = wide_rows.reshape(wide_rows.shape[:-1] + (2, head_count, head_size))
    taken = jnp.take(shaped, chosen, axis=shaped.ndim - 2)
    moved = jnp.moveaxis(taken, shaped.ndim - 2, 0)
    return moved.reshape(moved.shape[:-2] + (2 * head_size,))


def attn_kernel(q_ref, kd_ref, vd_ref, ks_ref, vs_ref, o_ref, m_sc, l_sc, acc_sc, *, n_doc, n_self, blk, inv_root):
    phase = pl.program_id(1)
    j = pl.program_id(2)
    rows = q_ref.shape[0]

    @pl.when((phase == 0) & (j == 0))
    def _():
        m_sc[...] = jnp.full(m_sc.shape, -jnp.inf, jnp.float32)
        l_sc[...] = jnp.zeros(l_sc.shape, jnp.float32)
        acc_sc[...] = jnp.zeros(acc_sc.shape, jnp.float32)

    def scores(k_ref, first_key):
        s = lax.dot_general(q_ref[...], k_ref[...], (((1,), (1,)), ((), ())),
                            preferred_element_type=jnp.float32) * inv_root
        if first_key is None:
            return s
        t = lax.broadcasted_iota(jnp.int32, s.shape, 0)
        u = lax.broadcasted_iota(jnp.int32, s.shape, 1) + first_key
        return jnp.where(u <= t, s, -jnp.inf)

    def step(k_ref, v_ref, first_key):
        @pl.when(phase == 0)
        def _():
            s = scores(k_ref, first_key)
            m_sc[...] = jnp.maximum(m_sc[...], jnp.max(s, axis=1, keepdims=True))

        @pl.when(phase == 1)
        def _():
            s = scores(k_ref, first_key)
            e = jnp.exp(s - m_sc[:, :1])
            l_sc[...] = l_sc[...] + jnp.sum(e, axis=1, keepdims=True)
            acc_sc[...] = acc_sc[...] + jnp.dot(e.astype(jnp.bfloat16), v_ref[...],
                                                preferred_element_type=jnp.float32)

    @pl.when(j < n_doc)
    def _():
        step(kd_ref, vd_ref, None)

    for b in range(n_self):
        @pl.when(j == n_doc + b)
        def _(b=b):
            step(ks_ref, vs_ref, b * blk)

    @pl.when((phase == 1) & (j == pl.num_programs(2) - 1))
    def _():
        o_ref[...] = (acc_sc[...] / l_sc[:, :1]).astype(o_ref.dtype)


def attention(q2d, blocks, own_self):
    T, width = q2d.shape
    heads = width // HD
    n_doc, blk, _ = blocks.shape
    n_self = T // blk
    last_doc = n_doc - 1
    kern = functools.partial(attn_kernel, n_doc=n_doc, n_self=n_self, blk=blk, inv_root=1.0 / math.sqrt(HD))
    doc_at = lambda j: jnp.minimum(j, last_doc)
    self_at = lambda j: jnp.maximum(j - n_doc, 0)
    return pl.pallas_call(
        kern,
        grid=(heads, 2, n_doc + n_self),
        in_specs=[
            pl.BlockSpec((T, HD), lambda h, p, j: (0, h)),
            pl.BlockSpec((None, blk, HD), lambda h, p, j: (doc_at(j), 0, 0)),
            pl.BlockSpec((None, blk, HD), lambda h, p, j: (doc_at(j), 0, 1)),
            pl.BlockSpec((blk, HD), lambda h, p, j: (self_at(j), 0)),
            pl.BlockSpec((blk, HD), lambda h, p, j: (self_at(j), 1)),
        ],
        out_specs=pl.BlockSpec((T, HD), lambda h, p, j: (0, h)),
        out_shape=jax.ShapeDtypeStruct((T, width), q2d.dtype),
        scratch_shapes=[pltpu.VMEM((T, HD), jnp.float32)] * 3,
    )(q2d, blocks, blocks, own_self, own_self)


def pair_sum(value, axis):
    size = lax.axis_size(axis)
    step = 1
    while step < size:
        value = value + lax.ppermute(value, axis, [(i, i ^ step) for i in range(size)])
        step *= 2
    return value


def halve_sum(value, axis):
    size = lax.axis_size(axis)
    me = lax.axis_index(axis)
    step = 1
    while step < size:
        bit = (me // step) % 2
        halves = value.reshape((2, value.shape[0] // 2) + value.shape[1:])
        keep = lax.dynamic_index_in_dim(halves, bit, 0, keepdims=False)
        send = lax.dynamic_index_in_dim(halves, 1 - bit, 0, keepdims=False)
        value = keep + lax.ppermute(send, axis, [(i, i ^ step) for i in range(size)])
        step *= 2
    return value


def double_gather(value, axis):
    size = lax.axis_size(axis)
    me = lax.axis_index(axis)
    step = size // 2
    while step >= 1:
        bit = (me // step) % 2
        other = lax.ppermute(value, axis, [(i, i ^ step) for i in range(size)])
        value = jnp.where(
            bit == 0, jnp.concatenate([value, other], axis=0), jnp.concatenate([other, value], axis=0)
        )
        step //= 2
    return value


def shards(queries, store_kv, self_kv, rec_states, norm_gain, w_kv, retrieval, doc_home, rec_index):
    groups = lax.axis_size("cache")
    members = lax.axis_size("dh") * lax.axis_size("dq")
    my_group = lax.axis_index("cache")
    my_member = lax.axis_index("dh") * lax.axis_size("dq") + lax.axis_index("dq")
    per_device = QH // members
    ratio_heads = QH // KVH
    my_head = my_member * per_device // ratio_heads
    shard_rows = store_kv.shape[1]
    kv_width = store_kv.shape[2]
    inv_root = 1.0 / math.sqrt(HD)
    stored_at = jnp.take(doc_home, retrieval, axis=0)
    source = stored_at // DOC_GRP
    local_row = stored_at % DOC_GRP
    before = jnp.arange(RET)[None, :] < jnp.arange(RET)[:, None]
    same_home = source[:, :, None] == source[:, None, :]
    rank_within = jnp.sum((same_home & before[None, :, :]).astype(jnp.int32), axis=2)
    places = jnp.arange(CAP, dtype=jnp.int32)
    matching = (source[:, None, :] == my_group) & (rank_within[:, None, :] == places[None, :, None])
    pick_row = jnp.sum(jnp.where(matching, local_row[:, None, :], 0), axis=2)
    filled = jnp.any(matching, axis=2)
    outgoing = jnp.take(store_kv, pick_row.reshape(-1), axis=0).reshape(
        groups, CAP, shard_rows, kv_width
    )
    outgoing = jnp.where(filled[:, :, None, None], outgoing, jnp.zeros((), store_kv.dtype))
    my_source = lax.dynamic_index_in_dim(source, my_group, 0, keepdims=False)
    my_rank = lax.dynamic_index_in_dim(rank_within, my_group, 0, keepdims=False)
    slot_place = my_source * CAP + my_rank
    dest_heads = jnp.arange(members, dtype=jnp.int32) * per_device // ratio_heads
    arrived = lax.all_to_all(outgoing, "cache", split_axis=0, concat_axis=0, tiled=True)
    compact = jnp.take(arrived.reshape(groups * CAP, shard_rows, kv_width), slot_place, axis=0)
    spread = pick_heads(compact, KVH, HD, dest_heads)
    fetched = lax.all_to_all(spread, ("dh", "dq"), split_axis=0, concat_axis=2, tiled=True)[0]
    states = rec_states[0].astype(jnp.float32)
    rows_rec = states.shape[0]
    partial_sq = jnp.sum(states * states, axis=1)
    total_sq = pair_sum(pair_sum(partial_sq, "dq"), "dh")
    inv_rms = lax.rsqrt(total_sq / D + eps_norm)
    normed = (states * norm_gain.astype(jnp.float32)[None, :] * inv_rms[:, None]).astype(jnp.bfloat16)
    partial_kv = jnp.dot(normed, w_kv, preferred_element_type=jnp.float32)
    row_part = halve_sum(partial_kv, "dq")
    fetched, row_part = lax.optimization_barrier((fetched, row_part))
    part_rows = row_part.shape[0]
    by_head = jnp.transpose(row_part.reshape(part_rows, 2, KVH, HD), (2, 0, 1, 3))
    head_parts = lax.all_to_all(by_head, "dh", split_axis=0, concat_axis=0, tiled=True)
    head_rows = jnp.sum(head_parts, axis=0).reshape(part_rows, 2 * HD).astype(jnp.bfloat16)
    redone = double_gather(head_rows, "dq")
    own_rows = redone.reshape(RET, REC, 2 * HD)
    full_block = fetched.shape[1]
    positions = rec_index[0]
    onehot = positions[:, :, None] == jnp.arange(full_block, dtype=jnp.int32)[None, None, :]
    placed = jnp.einsum(
        "kib,kic->kbc", onehot.astype(jnp.bfloat16), own_rows, preferred_element_type=jnp.float32
    ).astype(jnp.bfloat16)
    replaced_at = jnp.any(onehot, axis=1)
    blocks = jnp.where(replaced_at[:, :, None], placed, fetched)
    own_self = own_head(self_kv[0], KVH, HD, my_head)
    return attention(queries[0], blocks, own_self)[None]


def solution(mesh):
    dev = ("dh", "dq")
    groups = mesh.shape["cache"]
    members = mesh.shape["dev"]
    view = Mesh(mesh.devices.reshape(groups, KVH, members // KVH), ("cache", "dh", "dq"))
    placed = (
        P("cache", None, dev),
        P("cache", dev, None),
        P("cache", None, None),
        P("cache", None, dev),
        P(dev),
        P(dev, None),
        P(),
        P(),
        P("cache", None, None),
    )
    return jax.shard_map(
        shards, mesh=view, in_specs=placed, out_specs=P("cache", None, dev), check_vma=False
    )
```

```python
import functools
import math

import jax
import jax.numpy as jnp
from jax import lax
from jax.experimental import pallas as pl
from jax.experimental.pallas import tpu as pltpu
from jax.sharding import Mesh, PartitionSpec as P

D = 8192
QH = 64
KVH = 8
HD = 128
RET = 16
CAP = 4
REC = 32
DOC_GRP = 32


eps_norm = 1e-05
tile_rows = 512


def own_head(wide_rows, head_count, head_size, chosen):
    shaped = wide_rows.reshape(wide_rows.shape[:-1] + (2, head_count, head_size))
    taken = lax.dynamic_index_in_dim(shaped, chosen, shaped.ndim - 2, keepdims=False)
    return taken.reshape(wide_rows.shape[:-1] + (2 * head_size,))


def pick_heads(wide_rows, head_count, head_size, chosen):
    shaped = wide_rows.reshape(wide_rows.shape[:-1] + (2, head_count, head_size))
    taken = jnp.take(shaped, chosen, axis=shaped.ndim - 2)
    moved = jnp.moveaxis(taken, shaped.ndim - 2, 0)
    return moved.reshape(moved.shape[:-2] + (2 * head_size,))


def attn_kernel(q_ref, kd_ref, vd_ref, ks_ref, vs_ref, o_ref, m_sc, l_sc, acc_sc, *, n_doc, n_self, blk_self, inv_root):
    phase = pl.program_id(1)
    j = pl.program_id(2)

    @pl.when((phase == 0) & (j == 0))
    def _():
        m_sc[...] = jnp.full(m_sc.shape, -jnp.inf, jnp.float32)
        l_sc[...] = jnp.zeros(l_sc.shape, jnp.float32)
        acc_sc[...] = jnp.zeros(acc_sc.shape, jnp.float32)

    def raw(k_ref):
        return lax.dot_general(q_ref[...], k_ref[...], (((1,), (1,)), ((), ())), preferred_element_type=jnp.float32)

    def mask(s, first_key):
        if first_key is None:
            return s
        t = lax.broadcasted_iota(jnp.int32, s.shape, 0)
        u = lax.broadcasted_iota(jnp.int32, s.shape, 1) + first_key
        return jnp.where(u <= t, s, -jnp.inf)

    def step(k_ref, v_ref, first_key):
        @pl.when(phase == 0)
        def _():
            s = mask(raw(k_ref) * inv_root, first_key)
            m_sc[...] = jnp.maximum(m_sc[...], jnp.max(s, axis=1, keepdims=True))

        @pl.when(phase == 1)
        def _():
            s = mask(raw(k_ref) * inv_root, first_key)
            e = jnp.exp(s - m_sc[:, :1])
            eb = e.astype(jnp.bfloat16)
            l_sc[...] = l_sc[...] + jnp.sum(e, axis=1, keepdims=True)
            acc_sc[...] = acc_sc[...] + jnp.dot(eb, v_ref[...], preferred_element_type=jnp.float32)

    @pl.when(j < n_doc)
    def _():
        step(kd_ref, vd_ref, None)

    for b in range(n_self):
        @pl.when(j == n_doc + b)
        def _(b=b):
            step(ks_ref, vs_ref, b * blk_self)

    @pl.when((phase == 1) & (j == pl.num_programs(2) - 1))
    def _():
        o_ref[...] = (acc_sc[...] / l_sc[...][:, :1]).astype(o_ref.dtype)


def attention(q2d, blocks, own_self, bk=2048):
    T, width = q2d.shape
    heads = width // HD
    flat = blocks.reshape(-1, blocks.shape[-1])
    n_doc = flat.shape[0] // bk
    bs = min(bk, T)
    n_self = T // bs
    kern = functools.partial(attn_kernel, n_doc=n_doc, n_self=n_self, blk_self=bs, inv_root=1.0 / math.sqrt(HD))
    doc_at = lambda j: jnp.minimum(j, n_doc - 1)
    self_at = lambda j: jnp.maximum(j - n_doc, 0)
    kd_spec = pl.BlockSpec((bk, HD), lambda h, p, j: (doc_at(j), 0))
    ks_spec = pl.BlockSpec((bs, HD), lambda h, p, j: (self_at(j), 0))
    return pl.pallas_call(
        kern,
        grid=(heads, 2, n_doc + n_self),
        in_specs=[
            pl.BlockSpec((T, HD), lambda h, p, j: (0, h)),
            kd_spec,
            pl.BlockSpec((bk, HD), lambda h, p, j: (doc_at(j), 1)),
            ks_spec,
            pl.BlockSpec((bs, HD), lambda h, p, j: (self_at(j), 1)),
        ],
        out_specs=pl.BlockSpec((T, HD), lambda h, p, j: (0, h)),
        out_shape=jax.ShapeDtypeStruct((T, width), q2d.dtype),
        scratch_shapes=[pltpu.VMEM((T, HD), jnp.float32)] * 3,
    )(q2d, flat, flat, own_self, own_self)


def pair_sum(value, axis):
    size = lax.axis_size(axis)
    step = 1
    while step < size:
        value = value + lax.ppermute(value, axis, [(i, i ^ step) for i in range(size)])
        step *= 2
    return value


def halve_sum(value, axis):
    size = lax.axis_size(axis)
    me = lax.axis_index(axis)
    step = 1
    while step < size:
        bit = (me // step) % 2
        halves = value.reshape((2, value.shape[0] // 2) + value.shape[1:])
        keep = lax.dynamic_index_in_dim(halves, bit, 0, keepdims=False)
        send = lax.dynamic_index_in_dim(halves, 1 - bit, 0, keepdims=False)
        value = keep + lax.ppermute(send, axis, [(i, i ^ step) for i in range(size)])
        step *= 2
    return value


def double_gather(value, axis):
    size = lax.axis_size(axis)
    me = lax.axis_index(axis)
    step = size // 2
    while step >= 1:
        bit = (me // step) % 2
        other = lax.ppermute(value, axis, [(i, i ^ step) for i in range(size)])
        value = jnp.where(
            bit == 0, jnp.concatenate([value, other], axis=0), jnp.concatenate([other, value], axis=0)
        )
        step //= 2
    return value


def shards(queries, store_kv, self_kv, rec_states, norm_gain, w_kv, retrieval, doc_home, rec_index):
    groups = lax.axis_size("cache")
    members = lax.axis_size("dh") * lax.axis_size("dq")
    my_group = lax.axis_index("cache")
    my_member = lax.axis_index("dh") * lax.axis_size("dq") + lax.axis_index("dq")
    per_device = QH // members
    ratio_heads = QH // KVH
    my_head = my_member * per_device // ratio_heads
    shard_rows = store_kv.shape[1]
    kv_width = store_kv.shape[2]
    inv_root = 1.0 / math.sqrt(HD)
    stored_at = jnp.take(doc_home, retrieval, axis=0)
    source = stored_at // DOC_GRP
    local_row = stored_at % DOC_GRP
    before = jnp.arange(RET)[None, :] < jnp.arange(RET)[:, None]
    same_home = source[:, :, None] == source[:, None, :]
    rank_within = jnp.sum((same_home & before[None, :, :]).astype(jnp.int32), axis=2)
    places = jnp.arange(CAP, dtype=jnp.int32)
    matching = (source[:, None, :] == my_group) & (rank_within[:, None, :] == places[None, :, None])
    pick_row = jnp.sum(jnp.where(matching, local_row[:, None, :], 0), axis=2)
    filled = jnp.any(matching, axis=2)
    outgoing = jnp.take(store_kv, pick_row.reshape(-1), axis=0).reshape(
        groups, CAP, shard_rows, kv_width
    )
    outgoing = jnp.where(filled[:, :, None, None], outgoing, jnp.zeros((), store_kv.dtype))
    my_source = lax.dynamic_index_in_dim(source, my_group, 0, keepdims=False)
    my_rank = lax.dynamic_index_in_dim(rank_within, my_group, 0, keepdims=False)
    slot_place = my_source * CAP + my_rank
    dest_heads = jnp.arange(members, dtype=jnp.int32) * per_device // ratio_heads
    arrived = lax.all_to_all(outgoing, "cache", split_axis=0, concat_axis=0, tiled=True)
    compact = jnp.take(arrived.reshape(groups * CAP, shard_rows, kv_width), slot_place, axis=0)
    spread = pick_heads(compact, KVH, HD, dest_heads)
    fetched = lax.all_to_all(spread, ("dh", "dq"), split_axis=0, concat_axis=2, tiled=True)[0]
    states = rec_states[0].astype(jnp.float32)
    rows_rec = states.shape[0]
    partial_sq = jnp.sum(states * states, axis=1)
    total_sq = pair_sum(pair_sum(partial_sq, "dq"), "dh")
    inv_rms = lax.rsqrt(total_sq / D + eps_norm)
    normed = (states * norm_gain.astype(jnp.float32)[None, :] * inv_rms[:, None]).astype(jnp.bfloat16)
    partial_kv = jnp.dot(normed, w_kv, preferred_element_type=jnp.float32)
    row_part = halve_sum(partial_kv, "dq")
    part_rows = row_part.shape[0]
    by_head = jnp.transpose(row_part.reshape(part_rows, 2, KVH, HD), (2, 0, 1, 3))
    head_parts = lax.all_to_all(by_head, "dh", split_axis=0, concat_axis=0, tiled=True)
    head_rows = jnp.sum(head_parts, axis=0).reshape(part_rows, 2 * HD).astype(jnp.bfloat16)
    redone = double_gather(head_rows, "dq")
    own_rows = redone.reshape(RET, REC, 2 * HD)
    full_block = fetched.shape[1]
    positions = rec_index[0]
    onehot = positions[:, :, None] == jnp.arange(full_block, dtype=jnp.int32)[None, None, :]
    placed = jnp.einsum(
        "kib,kic->kbc", onehot.astype(jnp.bfloat16), own_rows, preferred_element_type=jnp.float32
    ).astype(jnp.bfloat16)
    replaced_at = jnp.any(onehot, axis=1)
    blocks = jnp.where(replaced_at[:, :, None], placed, fetched)
    own_self = own_head(self_kv[0], KVH, HD, my_head)
    return attention(queries[0], blocks, own_self)[None]


def solution(mesh):
    dev = ("dh", "dq")
    groups = mesh.shape["cache"]
    members = mesh.shape["dev"]
    view = Mesh(mesh.devices.reshape(groups, KVH, members // KVH), ("cache", "dh", "dq"))
    placed = (
        P("cache", None, dev),
        P("cache", dev, None),
        P("cache", None, None),
        P("cache", None, dev),
        P(dev),
        P(dev, None),
        P(),
        P(),
        P("cache", None, None),
    )
    return jax.shard_map(
        shards, mesh=view, in_specs=placed, out_specs=P("cache", None, dev), check_vma=False
    )
```

```python
import functools
import math

import jax
import jax.numpy as jnp
from jax import lax
from jax.experimental import pallas as pl
from jax.experimental.pallas import tpu as pltpu
from jax.sharding import Mesh, PartitionSpec as P

D = 8192
QH = 64
KVH = 8
HD = 128
RET = 16
CAP = 4
REC = 32
DOC_GRP = 32


eps_norm = 1e-05
tile_rows = 512


def own_head(wide_rows, head_count, head_size, chosen):
    shaped = wide_rows.reshape(wide_rows.shape[:-1] + (2, head_count, head_size))
    taken = lax.dynamic_index_in_dim(shaped, chosen, shaped.ndim - 2, keepdims=False)
    return taken.reshape(wide_rows.shape[:-1] + (2 * head_size,))


def pick_heads(wide_rows, head_count, head_size, chosen):
    shaped = wide_rows.reshape(wide_rows.shape[:-1] + (2, head_count, head_size))
    taken = jnp.take(shaped, chosen, axis=shaped.ndim - 2)
    moved = jnp.moveaxis(taken, shaped.ndim - 2, 0)
    return moved.reshape(moved.shape[:-2] + (2 * head_size,))


def attn_kernel(q_ref, kd_ref, vd_ref, ks_ref, vs_ref, o_ref, m_sc, l_sc, acc_sc, *, n_doc, n_self, blk_self, inv_root, heads):
    phase = pl.program_id(0)
    j = pl.program_id(1)

    @pl.when((phase == 0) & (j == 0))
    def _():
        m_sc[...] = jnp.full(m_sc.shape, -jnp.inf, jnp.float32)
        l_sc[...] = jnp.zeros(l_sc.shape, jnp.float32)
        acc_sc[...] = jnp.zeros(acc_sc.shape, jnp.float32)

    def scores(h, k_ref, first_key):
        q = q_ref[:, h * HD:(h + 1) * HD]
        s = lax.dot_general(q, k_ref[...], (((1,), (1,)), ((), ())), preferred_element_type=jnp.float32) * inv_root
        if first_key is None:
            return s
        t = lax.broadcasted_iota(jnp.int32, s.shape, 0)
        u = lax.broadcasted_iota(jnp.int32, s.shape, 1) + first_key
        return jnp.where(u <= t, s, -jnp.inf)

    def step(k_ref, v_ref, first_key):
        @pl.when(phase == 0)
        def _():
            for h in range(heads):
                s = scores(h, k_ref, first_key)
                m_sc[h] = jnp.maximum(m_sc[h], jnp.max(s, axis=1, keepdims=True))

        @pl.when(phase == 1)
        def _():
            for h in range(heads):
                s = scores(h, k_ref, first_key)
                e = jnp.exp(s - m_sc[h][:, :1])
                l_sc[h] = l_sc[h] + jnp.sum(e, axis=1, keepdims=True)
                acc_sc[h] = acc_sc[h] + jnp.dot(e.astype(jnp.bfloat16), v_ref[...], preferred_element_type=jnp.float32)

    @pl.when(j < n_doc)
    def _():
        step(kd_ref, vd_ref, None)

    for b in range(n_self):
        @pl.when(j == n_doc + b)
        def _(b=b):
            step(ks_ref, vs_ref, b * blk_self)

    @pl.when((phase == 1) & (j == pl.num_programs(1) - 1))
    def _():
        for h in range(heads):
            o_ref[:, h * HD:(h + 1) * HD] = (acc_sc[h] / l_sc[h][:, :1]).astype(o_ref.dtype)


def attention(q2d, blocks, own_self, bk=2048):
    T, width = q2d.shape
    heads = width // HD
    flat = blocks.reshape(-1, blocks.shape[-1])
    n_doc = flat.shape[0] // bk
    bs = min(bk, T)
    n_self = T // bs
    kern = functools.partial(attn_kernel, n_doc=n_doc, n_self=n_self, blk_self=bs, inv_root=1.0 / math.sqrt(HD), heads=heads)
    doc_at = lambda j: jnp.minimum(j, n_doc - 1)
    self_at = lambda j: jnp.maximum(j - n_doc, 0)
    return pl.pallas_call(
        kern,
        grid=(2, n_doc + n_self),
        in_specs=[
            pl.BlockSpec((T, width), lambda p, j: (0, 0)),
            pl.BlockSpec((bk, HD), lambda p, j: (doc_at(j), 0)),
            pl.BlockSpec((bk, HD), lambda p, j: (doc_at(j), 1)),
            pl.BlockSpec((bs, HD), lambda p, j: (self_at(j), 0)),
            pl.BlockSpec((bs, HD), lambda p, j: (self_at(j), 1)),
        ],
        out_specs=pl.BlockSpec((T, width), lambda p, j: (0, 0)),
        out_shape=jax.ShapeDtypeStruct((T, width), q2d.dtype),
        scratch_shapes=[pltpu.VMEM((heads, T, HD), jnp.float32)] * 3,
    )(q2d, flat, flat, own_self, own_self)


def pair_sum(value, axis):
    size = lax.axis_size(axis)
    step = 1
    while step < size:
        value = value + lax.ppermute(value, axis, [(i, i ^ step) for i in range(size)])
        step *= 2
    return value


def halve_sum(value, axis):
    size = lax.axis_size(axis)
    me = lax.axis_index(axis)
    step = 1
    while step < size:
        bit = (me // step) % 2
        halves = value.reshape((2, value.shape[0] // 2) + value.shape[1:])
        keep = lax.dynamic_index_in_dim(halves, bit, 0, keepdims=False)
        send = lax.dynamic_index_in_dim(halves, 1 - bit, 0, keepdims=False)
        value = keep + lax.ppermute(send, axis, [(i, i ^ step) for i in range(size)])
        step *= 2
    return value


def double_gather(value, axis):
    size = lax.axis_size(axis)
    me = lax.axis_index(axis)
    step = size // 2
    while step >= 1:
        bit = (me // step) % 2
        other = lax.ppermute(value, axis, [(i, i ^ step) for i in range(size)])
        value = jnp.where(
            bit == 0, jnp.concatenate([value, other], axis=0), jnp.concatenate([other, value], axis=0)
        )
        step //= 2
    return value


def shards(queries, store_kv, self_kv, rec_states, norm_gain, w_kv, retrieval, doc_home, rec_index):
    groups = lax.axis_size("cache")
    members = lax.axis_size("dh") * lax.axis_size("dq")
    my_group = lax.axis_index("cache")
    my_member = lax.axis_index("dh") * lax.axis_size("dq") + lax.axis_index("dq")
    per_device = QH // members
    ratio_heads = QH // KVH
    my_head = my_member * per_device // ratio_heads
    shard_rows = store_kv.shape[1]
    kv_width = store_kv.shape[2]
    inv_root = 1.0 / math.sqrt(HD)
    stored_at = jnp.take(doc_home, retrieval, axis=0)
    source = stored_at // DOC_GRP
    local_row = stored_at % DOC_GRP
    before = jnp.arange(RET)[None, :] < jnp.arange(RET)[:, None]
    same_home = source[:, :, None] == source[:, None, :]
    rank_within = jnp.sum((same_home & before[None, :, :]).astype(jnp.int32), axis=2)
    places = jnp.arange(CAP, dtype=jnp.int32)
    matching = (source[:, None, :] == my_group) & (rank_within[:, None, :] == places[None, :, None])
    pick_row = jnp.sum(jnp.where(matching, local_row[:, None, :], 0), axis=2)
    filled = jnp.any(matching, axis=2)
    outgoing = jnp.take(store_kv, pick_row.reshape(-1), axis=0).reshape(
        groups, CAP, shard_rows, kv_width
    )
    outgoing = jnp.where(filled[:, :, None, None], outgoing, jnp.zeros((), store_kv.dtype))
    my_source = lax.dynamic_index_in_dim(source, my_group, 0, keepdims=False)
    my_rank = lax.dynamic_index_in_dim(rank_within, my_group, 0, keepdims=False)
    slot_place = my_source * CAP + my_rank
    dest_heads = jnp.arange(members, dtype=jnp.int32) * per_device // ratio_heads
    arrived = lax.all_to_all(outgoing, "cache", split_axis=0, concat_axis=0, tiled=True)
    compact = jnp.take(arrived.reshape(groups * CAP, shard_rows, kv_width), slot_place, axis=0)
    spread = pick_heads(compact, KVH, HD, dest_heads)
    fetched = lax.all_to_all(spread, ("dh", "dq"), split_axis=0, concat_axis=2, tiled=True)[0]
    states = rec_states[0].astype(jnp.float32)
    rows_rec = states.shape[0]
    partial_sq = jnp.sum(states * states, axis=1)
    sq_rows = jnp.broadcast_to(partial_sq[None, :], (members, rows_rec))
    total_sq = jnp.sum(lax.all_to_all(sq_rows, ("dh", "dq"), split_axis=0, concat_axis=0, tiled=True), axis=0)
    inv_rms = lax.rsqrt(total_sq / D + eps_norm)
    normed = (states * norm_gain.astype(jnp.float32)[None, :] * inv_rms[:, None]).astype(jnp.bfloat16)
    partial_kv = jnp.dot(normed, w_kv, preferred_element_type=jnp.float32)
    row_part = halve_sum(partial_kv, "dq")
    part_rows = row_part.shape[0]
    by_head = jnp.transpose(row_part.reshape(part_rows, 2, KVH, HD), (2, 0, 1, 3))
    head_parts = lax.all_to_all(by_head, "dh", split_axis=0, concat_axis=0, tiled=True)
    head_rows = jnp.sum(head_parts, axis=0).reshape(part_rows, 2 * HD).astype(jnp.bfloat16)
    redone = double_gather(head_rows, "dq")
    own_rows = redone.reshape(RET, REC, 2 * HD)
    full_block = fetched.shape[1]
    positions = rec_index[0]
    onehot = positions[:, :, None] == jnp.arange(full_block, dtype=jnp.int32)[None, None, :]
    placed = jnp.einsum(
        "kib,kic->kbc", onehot.astype(jnp.bfloat16), own_rows, preferred_element_type=jnp.float32
    ).astype(jnp.bfloat16)
    replaced_at = jnp.any(onehot, axis=1)
    blocks = jnp.where(replaced_at[:, :, None], placed, fetched)
    own_self = own_head(self_kv[0], KVH, HD, my_head)
    return attention(queries[0], blocks, own_self)[None]


def solution(mesh):
    dev = ("dh", "dq")
    groups = mesh.shape["cache"]
    members = mesh.shape["dev"]
    view = Mesh(mesh.devices.reshape(groups, KVH, members // KVH), ("cache", "dh", "dq"))
    placed = (
        P("cache", None, dev),
        P("cache", dev, None),
        P("cache", None, None),
        P("cache", None, dev),
        P(dev),
        P(dev, None),
        P(),
        P(),
        P("cache", None, None),
    )
    return jax.shard_map(
        shards, mesh=view, in_specs=placed, out_specs=P("cache", None, dev), check_vma=False
    )
```

```python
import functools
import math

import jax
import jax.numpy as jnp
from jax import lax
from jax.experimental import pallas as pl
from jax.experimental.pallas import tpu as pltpu
from jax.sharding import Mesh, PartitionSpec as P

D = 8192
QH = 64
KVH = 8
HD = 128
RET = 16
CAP = 4
REC = 32
DOC_GRP = 32


eps_norm = 1e-05
tile_rows = 512


def own_head(wide_rows, head_count, head_size, chosen):
    shaped = wide_rows.reshape(wide_rows.shape[:-1] + (2, head_count, head_size))
    taken = lax.dynamic_index_in_dim(shaped, chosen, shaped.ndim - 2, keepdims=False)
    return taken.reshape(wide_rows.shape[:-1] + (2 * head_size,))


def pick_heads(wide_rows, head_count, head_size, chosen):
    shaped = wide_rows.reshape(wide_rows.shape[:-1] + (2, head_count, head_size))
    taken = jnp.take(shaped, chosen, axis=shaped.ndim - 2)
    moved = jnp.moveaxis(taken, shaped.ndim - 2, 0)
    return moved.reshape(moved.shape[:-2] + (2 * head_size,))


def attn_kernel(q_ref, kd_ref, vd_ref, kp_ref, vp_ref, fl_ref, ks_ref, vs_ref, o_ref, m_sc, l_sc, acc_sc, *, n_doc, n_self, blk_self, inv_root, heads):
    phase = pl.program_id(0)
    j = pl.program_id(1)

    @pl.when((phase == 0) & (j == 0))
    def _():
        m_sc[...] = jnp.full(m_sc.shape, -jnp.inf, jnp.float32)
        l_sc[...] = jnp.zeros(l_sc.shape, jnp.float32)
        acc_sc[...] = jnp.zeros(acc_sc.shape, jnp.float32)

    def scores(h, keys, first_key):
        q = q_ref[:, h * HD:(h + 1) * HD]
        s = lax.dot_general(q, keys, (((1,), (1,)), ((), ())), preferred_element_type=jnp.float32) * inv_root
        if first_key is None:
            return s
        t = lax.broadcasted_iota(jnp.int32, s.shape, 0)
        u = lax.broadcasted_iota(jnp.int32, s.shape, 1) + first_key
        return jnp.where(u <= t, s, -jnp.inf)

    def step(get_keys, get_values, first_key):
        @pl.when(phase == 0)
        def _():
            keys = get_keys()
            for h in range(heads):
                s = scores(h, keys, first_key)
                m_sc[h] = jnp.maximum(m_sc[h], jnp.max(s, axis=1, keepdims=True))

        @pl.when(phase == 1)
        def _():
            keys = get_keys()
            values = get_values()
            for h in range(heads):
                s = scores(h, keys, first_key)
                e = jnp.exp(s - m_sc[h][:, :1])
                l_sc[h] = l_sc[h] + jnp.sum(e, axis=1, keepdims=True)
                acc_sc[h] = acc_sc[h] + jnp.dot(e.astype(jnp.bfloat16), values, preferred_element_type=jnp.float32)

    def merged(placed_ref, stored_ref):
        return jnp.where(fl_ref[...] != 0, placed_ref[...], stored_ref[...])

    @pl.when(j < n_doc)
    def _():
        step(lambda: merged(kp_ref, kd_ref), lambda: merged(vp_ref, vd_ref), None)

    for b in range(n_self):
        @pl.when(j == n_doc + b)
        def _(b=b):
            step(lambda: ks_ref[...], lambda: vs_ref[...], b * blk_self)

    @pl.when((phase == 1) & (j == pl.num_programs(1) - 1))
    def _():
        for h in range(heads):
            o_ref[:, h * HD:(h + 1) * HD] = (acc_sc[h] / l_sc[h][:, :1]).astype(o_ref.dtype)


def attention(q2d, flat, placed, flags, own_self, bk=2048):
    T, width = q2d.shape
    heads = width // HD
    n_doc = flat.shape[0] // bk
    bs = min(bk, T)
    n_self = T // bs
    kern = functools.partial(attn_kernel, n_doc=n_doc, n_self=n_self, blk_self=bs, inv_root=1.0 / math.sqrt(HD), heads=heads)
    doc_at = lambda j: jnp.minimum(j, n_doc - 1)
    self_at = lambda j: jnp.maximum(j - n_doc, 0)
    return pl.pallas_call(
        kern,
        grid=(2, n_doc + n_self),
        in_specs=[
            pl.BlockSpec((T, width), lambda p, j: (0, 0)),
            pl.BlockSpec((bk, HD), lambda p, j: (doc_at(j), 0)),
            pl.BlockSpec((bk, HD), lambda p, j: (doc_at(j), 1)),
            pl.BlockSpec((bk, HD), lambda p, j: (doc_at(j), 0)),
            pl.BlockSpec((bk, HD), lambda p, j: (doc_at(j), 1)),
            pl.BlockSpec((bk, 1), lambda p, j: (doc_at(j), 0)),
            pl.BlockSpec((bs, HD), lambda p, j: (self_at(j), 0)),
            pl.BlockSpec((bs, HD), lambda p, j: (self_at(j), 1)),
        ],
        out_specs=pl.BlockSpec((T, width), lambda p, j: (0, 0)),
        out_shape=jax.ShapeDtypeStruct((T, width), q2d.dtype),
        scratch_shapes=[pltpu.VMEM((heads, T, HD), jnp.float32)] * 3,
    )(q2d, flat, flat, placed, placed, flags, own_self, own_self)


def pair_sum(value, axis):
    size = lax.axis_size(axis)
    step = 1
    while step < size:
        value = value + lax.ppermute(value, axis, [(i, i ^ step) for i in range(size)])
        step *= 2
    return value


def halve_sum(value, axis):
    size = lax.axis_size(axis)
    me = lax.axis_index(axis)
    step = 1
    while step < size:
        bit = (me // step) % 2
        halves = value.reshape((2, value.shape[0] // 2) + value.shape[1:])
        keep = lax.dynamic_index_in_dim(halves, bit, 0, keepdims=False)
        send = lax.dynamic_index_in_dim(halves, 1 - bit, 0, keepdims=False)
        value = keep + lax.ppermute(send, axis, [(i, i ^ step) for i in range(size)])
        step *= 2
    return value


def double_gather(value, axis):
    size = lax.axis_size(axis)
    me = lax.axis_index(axis)
    step = size // 2
    while step >= 1:
        bit = (me // step) % 2
        other = lax.ppermute(value, axis, [(i, i ^ step) for i in range(size)])
        value = jnp.where(
            bit == 0, jnp.concatenate([value, other], axis=0), jnp.concatenate([other, value], axis=0)
        )
        step //= 2
    return value


def shards(queries, store_kv, self_kv, rec_states, norm_gain, w_kv, retrieval, doc_home, rec_index):
    groups = lax.axis_size("cache")
    members = lax.axis_size("dh") * lax.axis_size("dq")
    my_group = lax.axis_index("cache")
    my_member = lax.axis_index("dh") * lax.axis_size("dq") + lax.axis_index("dq")
    per_device = QH // members
    ratio_heads = QH // KVH
    my_head = my_member * per_device // ratio_heads
    shard_rows = store_kv.shape[1]
    kv_width = store_kv.shape[2]
    inv_root = 1.0 / math.sqrt(HD)
    stored_at = jnp.take(doc_home, retrieval, axis=0)
    source = stored_at // DOC_GRP
    local_row = stored_at % DOC_GRP
    before = jnp.arange(RET)[None, :] < jnp.arange(RET)[:, None]
    same_home = source[:, :, None] == source[:, None, :]
    rank_within = jnp.sum((same_home & before[None, :, :]).astype(jnp.int32), axis=2)
    places = jnp.arange(CAP, dtype=jnp.int32)
    matching = (source[:, None, :] == my_group) & (rank_within[:, None, :] == places[None, :, None])
    pick_row = jnp.sum(jnp.where(matching, local_row[:, None, :], 0), axis=2)
    filled = jnp.any(matching, axis=2)
    outgoing = jnp.take(store_kv, pick_row.reshape(-1), axis=0).reshape(
        groups, CAP, shard_rows, kv_width
    )
    outgoing = jnp.where(filled[:, :, None, None], outgoing, jnp.zeros((), store_kv.dtype))
    my_source = lax.dynamic_index_in_dim(source, my_group, 0, keepdims=False)
    my_rank = lax.dynamic_index_in_dim(rank_within, my_group, 0, keepdims=False)
    slot_place = my_source * CAP + my_rank
    dest_heads = jnp.arange(members, dtype=jnp.int32) * per_device // ratio_heads
    arrived = lax.all_to_all(outgoing, "cache", split_axis=0, concat_axis=0, tiled=True)
    compact = jnp.take(arrived.reshape(groups * CAP, shard_rows, kv_width), slot_place, axis=0)
    spread = pick_heads(compact, KVH, HD, dest_heads)
    fetched = lax.all_to_all(spread, ("dh", "dq"), split_axis=0, concat_axis=0, tiled=True)
    states = rec_states[0].astype(jnp.float32)
    rows_rec = states.shape[0]
    partial_sq = jnp.sum(states * states, axis=1)
    sq_rows = jnp.broadcast_to(partial_sq[None, :], (members, rows_rec))
    total_sq = jnp.sum(lax.all_to_all(sq_rows, ("dh", "dq"), split_axis=0, concat_axis=0, tiled=True), axis=0)
    inv_rms = lax.rsqrt(total_sq / D + eps_norm)
    normed = (states * norm_gain.astype(jnp.float32)[None, :] * inv_rms[:, None]).astype(jnp.bfloat16)
    partial_kv = jnp.dot(normed, w_kv, preferred_element_type=jnp.float32)
    row_part = halve_sum(partial_kv, "dq")
    part_rows = row_part.shape[0]
    by_head = jnp.transpose(row_part.reshape(part_rows, 2, KVH, HD), (2, 0, 1, 3))
    head_parts = lax.all_to_all(by_head, "dh", split_axis=0, concat_axis=0, tiled=True)
    head_rows = jnp.sum(head_parts, axis=0).reshape(part_rows, 2 * HD).astype(jnp.bfloat16)
    redone = double_gather(head_rows, "dq")
    own_rows = redone.reshape(RET, REC, 2 * HD)
    positions = rec_index[0]
    shard_tokens = fetched.shape[2]
    spots = jnp.arange(members, dtype=jnp.int32)[:, None] * shard_tokens + jnp.arange(
        shard_tokens, dtype=jnp.int32
    )[None, :]
    onehot = positions[None, :, None, :] == spots[:, None, :, None]
    placed = jnp.einsum(
        "mkti,kic->mktc", onehot.astype(jnp.bfloat16), own_rows, preferred_element_type=jnp.float32
    ).astype(jnp.bfloat16)
    flags = jnp.any(onehot, axis=3).astype(jnp.int32).reshape(-1, 1)
    own_self = own_head(self_kv[0], KVH, HD, my_head)
    width = fetched.shape[-1]
    return attention(queries[0], fetched.reshape(-1, width), placed.reshape(-1, width), flags, own_self)[None]


def solution(mesh):
    dev = ("dh", "dq")
    groups = mesh.shape["cache"]
    members = mesh.shape["dev"]
    view = Mesh(mesh.devices.reshape(groups, KVH, members // KVH), ("cache", "dh", "dq"))
    placed = (
        P("cache", None, dev),
        P("cache", dev, None),
        P("cache", None, None),
        P("cache", None, dev),
        P(dev),
        P(dev, None),
        P(),
        P(),
        P("cache", None, None),
    )
    return jax.shard_map(
        shards, mesh=view, in_specs=placed, out_specs=P("cache", None, dev), check_vma=False
    )
```

```python
import functools
import math

import jax
import jax.numpy as jnp
from jax import lax
from jax.experimental import pallas as pl
from jax.experimental.pallas import tpu as pltpu
from jax.sharding import Mesh, PartitionSpec as P

D = 8192
QH = 64
KVH = 8
HD = 128
RET = 16
CAP = 4
REC = 32
DOC_GRP = 32


eps_norm = 1e-05
tile_rows = 512


def own_head(wide_rows, head_count, head_size, chosen):
    shaped = wide_rows.reshape(wide_rows.shape[:-1] + (2, head_count, head_size))
    taken = lax.dynamic_index_in_dim(shaped, chosen, shaped.ndim - 2, keepdims=False)
    return taken.reshape(wide_rows.shape[:-1] + (2 * head_size,))


def pick_heads(wide_rows, head_count, head_size, chosen):
    shaped = wide_rows.reshape(wide_rows.shape[:-1] + (2, head_count, head_size))
    taken = jnp.take(shaped, chosen, axis=shaped.ndim - 2)
    moved = jnp.moveaxis(taken, shaped.ndim - 2, 0)
    return moved.reshape(moved.shape[:-2] + (2 * head_size,))


def attn_kernel(q_ref, kd_ref, vd_ref, ks_ref, vs_ref, o_ref, m_sc, l_sc, acc_sc, *, n_doc, n_self, blk_self, inv_root, heads):
    phase = pl.program_id(0)
    j = pl.program_id(1)

    @pl.when((phase == 0) & (j == 0))
    def _():
        m_sc[...] = jnp.full(m_sc.shape, -jnp.inf, jnp.float32)
        l_sc[...] = jnp.zeros(l_sc.shape, jnp.float32)
        acc_sc[...] = jnp.zeros(acc_sc.shape, jnp.float32)

    def scores(h, k_ref, first_key):
        q = q_ref[:, h * HD:(h + 1) * HD]
        s = lax.dot_general(q, k_ref[...], (((1,), (1,)), ((), ())), preferred_element_type=jnp.float32) * inv_root
        if first_key is None:
            return s
        t = lax.broadcasted_iota(jnp.int32, s.shape, 0)
        u = lax.broadcasted_iota(jnp.int32, s.shape, 1) + first_key
        return jnp.where(u <= t, s, -jnp.inf)

    def step(k_ref, v_ref, first_key):
        @pl.when(phase == 0)
        def _():
            for h in range(heads):
                s = scores(h, k_ref, first_key)
                m_sc[h] = jnp.maximum(m_sc[h], jnp.max(s, axis=1, keepdims=True))

        @pl.when(phase == 1)
        def _():
            for h in range(heads):
                s = scores(h, k_ref, first_key)
                e = jnp.exp(s - m_sc[h][:, :1])
                l_sc[h] = l_sc[h] + jnp.sum(e, axis=1, keepdims=True)
                acc_sc[h] = acc_sc[h] + jnp.dot(e.astype(jnp.bfloat16), v_ref[...], preferred_element_type=jnp.float32)

    @pl.when(j < n_doc)
    def _():
        step(kd_ref, vd_ref, None)

    for b in range(n_self):
        @pl.when(j == n_doc + b)
        def _(b=b):
            step(ks_ref, vs_ref, b * blk_self)

    @pl.when((phase == 1) & (j == pl.num_programs(1) - 1))
    def _():
        for h in range(heads):
            o_ref[:, h * HD:(h + 1) * HD] = (acc_sc[h] / l_sc[h][:, :1]).astype(o_ref.dtype)


def attention(q2d, blocks, own_self, bk=2048):
    T, width = q2d.shape
    heads = width // HD
    flat = blocks.reshape(-1, blocks.shape[-1])
    n_doc = flat.shape[0] // bk
    bs = min(bk, T)
    n_self = T // bs
    kern = functools.partial(attn_kernel, n_doc=n_doc, n_self=n_self, blk_self=bs, inv_root=1.0 / math.sqrt(HD), heads=heads)
    doc_at = lambda j: jnp.minimum(j, n_doc - 1)
    self_at = lambda j: jnp.maximum(j - n_doc, 0)
    return pl.pallas_call(
        kern,
        grid=(2, n_doc + n_self),
        in_specs=[
            pl.BlockSpec((T, width), lambda p, j: (0, 0)),
            pl.BlockSpec((bk, HD), lambda p, j: (doc_at(j), 0)),
            pl.BlockSpec((bk, HD), lambda p, j: (doc_at(j), 1)),
            pl.BlockSpec((bs, HD), lambda p, j: (self_at(j), 0)),
            pl.BlockSpec((bs, HD), lambda p, j: (self_at(j), 1)),
        ],
        out_specs=pl.BlockSpec((T, width), lambda p, j: (0, 0)),
        out_shape=jax.ShapeDtypeStruct((T, width), q2d.dtype),
        scratch_shapes=[pltpu.VMEM((heads, T, HD), jnp.float32)] * 3,
    )(q2d, flat, flat, own_self, own_self)


def pair_sum(value, axis):
    size = lax.axis_size(axis)
    step = 1
    while step < size:
        value = value + lax.ppermute(value, axis, [(i, i ^ step) for i in range(size)])
        step *= 2
    return value


def halve_sum(value, axis, dim=0):
    size = lax.axis_size(axis)
    me = lax.axis_index(axis)
    step = 1
    while step < size:
        bit = (me // step) % 2
        shape = value.shape
        halves = value.reshape(shape[:dim] + (2, shape[dim] // 2) + shape[dim + 1 :])
        keep = lax.dynamic_index_in_dim(halves, bit, dim, keepdims=False)
        send = lax.dynamic_index_in_dim(halves, 1 - bit, dim, keepdims=False)
        value = keep + lax.ppermute(send, axis, [(i, i ^ step) for i in range(size)])
        step *= 2
    return value


def double_gather(value, axis):
    size = lax.axis_size(axis)
    me = lax.axis_index(axis)
    step = size // 2
    while step >= 1:
        bit = (me // step) % 2
        other = lax.ppermute(value, axis, [(i, i ^ step) for i in range(size)])
        value = jnp.where(
            bit == 0, jnp.concatenate([value, other], axis=0), jnp.concatenate([other, value], axis=0)
        )
        step //= 2
    return value


def shards(queries, store_kv, self_kv, rec_states, norm_gain, w_kv, retrieval, doc_home, rec_index):
    groups = lax.axis_size("cache")
    members = lax.axis_size("dh") * lax.axis_size("dq")
    my_group = lax.axis_index("cache")
    my_member = lax.axis_index("dh") * lax.axis_size("dq") + lax.axis_index("dq")
    per_device = QH // members
    ratio_heads = QH // KVH
    my_head = my_member * per_device // ratio_heads
    shard_rows = store_kv.shape[1]
    kv_width = store_kv.shape[2]
    inv_root = 1.0 / math.sqrt(HD)
    stored_at = jnp.take(doc_home, retrieval, axis=0)
    source = stored_at // DOC_GRP
    local_row = stored_at % DOC_GRP
    before = jnp.arange(RET)[None, :] < jnp.arange(RET)[:, None]
    same_home = source[:, :, None] == source[:, None, :]
    rank_within = jnp.sum((same_home & before[None, :, :]).astype(jnp.int32), axis=2)
    places = jnp.arange(CAP, dtype=jnp.int32)
    matching = (source[:, None, :] == my_group) & (rank_within[:, None, :] == places[None, :, None])
    pick_row = jnp.sum(jnp.where(matching, local_row[:, None, :], 0), axis=2)
    filled = jnp.any(matching, axis=2)
    outgoing = jnp.take(store_kv, pick_row.reshape(-1), axis=0).reshape(
        groups, CAP, shard_rows, kv_width
    )
    outgoing = jnp.where(filled[:, :, None, None], outgoing, jnp.zeros((), store_kv.dtype))
    my_source = lax.dynamic_index_in_dim(source, my_group, 0, keepdims=False)
    my_rank = lax.dynamic_index_in_dim(rank_within, my_group, 0, keepdims=False)
    slot_place = my_source * CAP + my_rank
    dest_heads = jnp.arange(members, dtype=jnp.int32) * per_device // ratio_heads
    arrived = lax.all_to_all(outgoing, "cache", split_axis=0, concat_axis=0, tiled=True)
    compact = jnp.take(arrived.reshape(groups * CAP, shard_rows, kv_width), slot_place, axis=0)
    spread = pick_heads(compact, KVH, HD, dest_heads)
    fetched = lax.all_to_all(spread, ("dh", "dq"), split_axis=0, concat_axis=2, tiled=True)[0]
    states = rec_states[0].astype(jnp.float32)
    rows_rec = states.shape[0]
    partial_sq = jnp.sum(states * states, axis=1)
    sq_rows = jnp.broadcast_to(partial_sq[None, :], (members, rows_rec))
    total_sq = jnp.sum(lax.all_to_all(sq_rows, ("dh", "dq"), split_axis=0, concat_axis=0, tiled=True), axis=0)
    inv_rms = lax.rsqrt(total_sq / D + eps_norm)
    normed = (states * norm_gain.astype(jnp.float32)[None, :] * inv_rms[:, None]).astype(jnp.bfloat16)
    partial_kv = jnp.dot(normed, w_kv, preferred_element_type=jnp.float32)
    kv_heads = jnp.transpose(partial_kv.reshape(rows_rec, 2, KVH, HD), (2, 0, 1, 3))
    by_head = halve_sum(kv_heads.reshape(KVH, rows_rec, 2 * HD), "dq", 1)
    part_rows = by_head.shape[1]
    head_parts = lax.all_to_all(by_head, "dh", split_axis=0, concat_axis=0, tiled=True)
    head_rows = jnp.sum(head_parts, axis=0).astype(jnp.bfloat16)
    redone = double_gather(head_rows, "dq")
    own_rows = redone.reshape(RET, REC, 2 * HD)
    full_block = fetched.shape[1]
    positions = rec_index[0]
    onehot = positions[:, :, None] == jnp.arange(full_block, dtype=jnp.int32)[None, None, :]
    placed = jnp.einsum(
        "kib,kic->kbc", onehot.astype(jnp.bfloat16), own_rows, preferred_element_type=jnp.float32
    ).astype(jnp.bfloat16)
    replaced_at = jnp.any(onehot, axis=1)
    blocks = jnp.where(replaced_at[:, :, None], placed, fetched)
    own_self = own_head(self_kv[0], KVH, HD, my_head)
    return attention(queries[0], blocks, own_self)[None]


def solution(mesh):
    dev = ("dh", "dq")
    groups = mesh.shape["cache"]
    members = mesh.shape["dev"]
    view = Mesh(mesh.devices.reshape(groups, KVH, members // KVH), ("cache", "dh", "dq"))
    placed = (
        P("cache", None, dev),
        P("cache", dev, None),
        P("cache", None, None),
        P("cache", None, dev),
        P(dev),
        P(dev, None),
        P(),
        P(),
        P("cache", None, None),
    )
    return jax.shard_map(
        shards, mesh=view, in_specs=placed, out_specs=P("cache", None, dev), check_vma=False
    )
```

```python
import functools
import math

import jax
import jax.numpy as jnp
from jax import lax
from jax.experimental import pallas as pl
from jax.experimental.pallas import tpu as pltpu
from jax.sharding import Mesh, PartitionSpec as P

D = 8192
QH = 64
KVH = 8
HD = 128
RET = 16
CAP = 4
REC = 32
DOC_GRP = 32
DEV = ("xh", "xl", "zh", "zq1", "zq0")


eps_norm = 1e-05
tile_rows = 512


def own_head(wide_rows, head_count, head_size, chosen):
    shaped = wide_rows.reshape(wide_rows.shape[:-1] + (2, head_count, head_size))
    taken = lax.dynamic_index_in_dim(shaped, chosen, shaped.ndim - 2, keepdims=False)
    return taken.reshape(wide_rows.shape[:-1] + (2 * head_size,))


def pick_heads(wide_rows, head_count, head_size, chosen):
    shaped = wide_rows.reshape(wide_rows.shape[:-1] + (2, head_count, head_size))
    taken = jnp.take(shaped, chosen, axis=shaped.ndim - 2)
    moved = jnp.moveaxis(taken, shaped.ndim - 2, 0)
    return moved.reshape(moved.shape[:-2] + (2 * head_size,))


def attn_kernel(q_ref, kd_ref, vd_ref, ks_ref, vs_ref, o_ref, m_sc, l_sc, acc_sc, *, n_doc, n_self, blk_self, inv_root, heads):
    phase = pl.program_id(0)
    j = pl.program_id(1)

    @pl.when((phase == 0) & (j == 0))
    def _():
        m_sc[...] = jnp.full(m_sc.shape, -jnp.inf, jnp.float32)
        l_sc[...] = jnp.zeros(l_sc.shape, jnp.float32)
        acc_sc[...] = jnp.zeros(acc_sc.shape, jnp.float32)

    def scores(h, k_ref, first_key):
        q = q_ref[:, h * HD:(h + 1) * HD]
        s = lax.dot_general(q, k_ref[...], (((1,), (1,)), ((), ())), preferred_element_type=jnp.float32) * inv_root
        if first_key is None:
            return s
        t = lax.broadcasted_iota(jnp.int32, s.shape, 0)
        u = lax.broadcasted_iota(jnp.int32, s.shape, 1) + first_key
        return jnp.where(u <= t, s, -jnp.inf)

    def step(k_ref, v_ref, first_key):
        @pl.when(phase == 0)
        def _():
            for h in range(heads):
                s = scores(h, k_ref, first_key)
                m_sc[h] = jnp.maximum(m_sc[h], jnp.max(s, axis=1, keepdims=True))

        @pl.when(phase == 1)
        def _():
            for h in range(heads):
                s = scores(h, k_ref, first_key)
                e = jnp.exp(s - m_sc[h][:, :1])
                l_sc[h] = l_sc[h] + jnp.sum(e, axis=1, keepdims=True)
                acc_sc[h] = acc_sc[h] + jnp.dot(e.astype(jnp.bfloat16), v_ref[...], preferred_element_type=jnp.float32)

    @pl.when(j < n_doc)
    def _():
        step(kd_ref, vd_ref, None)

    for b in range(n_self):
        @pl.when(j == n_doc + b)
        def _(b=b):
            step(ks_ref, vs_ref, b * blk_self)

    @pl.when((phase == 1) & (j == pl.num_programs(1) - 1))
    def _():
        for h in range(heads):
            o_ref[:, h * HD:(h + 1) * HD] = (acc_sc[h] / l_sc[h][:, :1]).astype(o_ref.dtype)


def attention(q2d, blocks, own_self, bk=2048):
    T, width = q2d.shape
    heads = width // HD
    flat = blocks.reshape(-1, blocks.shape[-1])
    n_doc = flat.shape[0] // bk
    bs = min(bk, T)
    n_self = T // bs
    kern = functools.partial(attn_kernel, n_doc=n_doc, n_self=n_self, blk_self=bs, inv_root=1.0 / math.sqrt(HD), heads=heads)
    doc_at = lambda j: jnp.minimum(j, n_doc - 1)
    self_at = lambda j: jnp.maximum(j - n_doc, 0)
    return pl.pallas_call(
        kern,
        grid=(2, n_doc + n_self),
        in_specs=[
            pl.BlockSpec((T, width), lambda p, j: (0, 0)),
            pl.BlockSpec((bk, HD), lambda p, j: (doc_at(j), 0)),
            pl.BlockSpec((bk, HD), lambda p, j: (doc_at(j), 1)),
            pl.BlockSpec((bs, HD), lambda p, j: (self_at(j), 0)),
            pl.BlockSpec((bs, HD), lambda p, j: (self_at(j), 1)),
        ],
        out_specs=pl.BlockSpec((T, width), lambda p, j: (0, 0)),
        out_shape=jax.ShapeDtypeStruct((T, width), q2d.dtype),
        scratch_shapes=[pltpu.VMEM((heads, T, HD), jnp.float32)] * 3,
    )(q2d, flat, flat, own_self, own_self)


def pair_sum(value, axis):
    size = lax.axis_size(axis)
    step = 1
    while step < size:
        value = value + lax.ppermute(value, axis, [(i, i ^ step) for i in range(size)])
        step *= 2
    return value


def halve_sum(value, axis, dim=0):
    size = lax.axis_size(axis)
    me = lax.axis_index(axis)
    step = 1
    while step < size:
        bit = (me // step) % 2
        shape = value.shape
        halves = value.reshape(shape[:dim] + (2, shape[dim] // 2) + shape[dim + 1 :])
        keep = lax.dynamic_index_in_dim(halves, bit, dim, keepdims=False)
        send = lax.dynamic_index_in_dim(halves, 1 - bit, dim, keepdims=False)
        value = keep + lax.ppermute(send, axis, [(i, i ^ step) for i in range(size)])
        step *= 2
    return value


def double_gather(value, axis):
    size = lax.axis_size(axis)
    me = lax.axis_index(axis)
    step = size // 2
    while step >= 1:
        bit = (me // step) % 2
        other = lax.ppermute(value, axis, [(i, i ^ step) for i in range(size)])
        value = jnp.where(
            bit == 0, jnp.concatenate([value, other], axis=0), jnp.concatenate([other, value], axis=0)
        )
        step //= 2
    return value


def shards(queries, store_kv, self_kv, rec_states, norm_gain, w_kv, retrieval, doc_home, rec_index):
    groups = lax.axis_size("cache")
    members = lax.axis_size(DEV)
    my_group = lax.axis_index("cache")
    my_member = lax.axis_index(DEV)
    per_device = QH // members
    ratio_heads = QH // KVH
    my_head = my_member * per_device // ratio_heads
    shard_rows = store_kv.shape[1]
    kv_width = store_kv.shape[2]
    inv_root = 1.0 / math.sqrt(HD)
    stored_at = jnp.take(doc_home, retrieval, axis=0)
    source = stored_at // DOC_GRP
    local_row = stored_at % DOC_GRP
    before = jnp.arange(RET)[None, :] < jnp.arange(RET)[:, None]
    same_home = source[:, :, None] == source[:, None, :]
    rank_within = jnp.sum((same_home & before[None, :, :]).astype(jnp.int32), axis=2)
    places = jnp.arange(CAP, dtype=jnp.int32)
    matching = (source[:, None, :] == my_group) & (rank_within[:, None, :] == places[None, :, None])
    pick_row = jnp.sum(jnp.where(matching, local_row[:, None, :], 0), axis=2)
    filled = jnp.any(matching, axis=2)
    outgoing = jnp.take(store_kv, pick_row.reshape(-1), axis=0).reshape(
        groups, CAP, shard_rows, kv_width
    )
    outgoing = jnp.where(filled[:, :, None, None], outgoing, jnp.zeros((), store_kv.dtype))
    my_source = lax.dynamic_index_in_dim(source, my_group, 0, keepdims=False)
    my_rank = lax.dynamic_index_in_dim(rank_within, my_group, 0, keepdims=False)
    slot_place = my_source * CAP + my_rank
    dest_heads = jnp.arange(members, dtype=jnp.int32) * per_device // ratio_heads
    arrived = lax.all_to_all(outgoing, "cache", split_axis=0, concat_axis=0, tiled=True)
    compact = jnp.take(arrived.reshape(groups * CAP, shard_rows, kv_width), slot_place, axis=0)
    spread = pick_heads(compact, KVH, HD, dest_heads)
    fetched = lax.all_to_all(spread, DEV, split_axis=0, concat_axis=2, tiled=True)[0]
    states = rec_states[0].astype(jnp.float32)
    rows_rec = states.shape[0]
    partial_sq = jnp.sum(states * states, axis=1)
    sq_rows = jnp.broadcast_to(partial_sq[None, :], (members, rows_rec))
    total_sq = jnp.sum(lax.all_to_all(sq_rows, DEV, split_axis=0, concat_axis=0, tiled=True), axis=0)
    inv_rms = lax.rsqrt(total_sq / D + eps_norm)
    normed = (states * norm_gain.astype(jnp.float32)[None, :] * inv_rms[:, None]).astype(jnp.bfloat16)
    partial_kv = jnp.dot(normed, w_kv, preferred_element_type=jnp.float32)
    row_part = halve_sum(partial_kv, "zq0")
    half_rows = row_part.shape[0]
    by_bits = row_part.reshape(half_rows, 2, 2, 2, 2, HD)
    head_part = halve_sum(by_bits, "xl", 3)
    part_rows = half_rows // 2
    by_dest = jnp.transpose(head_part.reshape(2, part_rows, 2, 2, 2, HD), (3, 4, 0, 1, 2, 5))
    by_dest = by_dest.reshape(KVH, part_rows, 2, HD)
    head_parts = lax.all_to_all(by_dest, ("xh", "zh", "zq1"), split_axis=0, concat_axis=0, tiled=True)
    head_rows = jnp.sum(head_parts, axis=0).reshape(part_rows, 2 * HD).astype(jnp.bfloat16)
    redone = double_gather(head_rows, ("zq1", "zq0"))
    own_rows = redone.reshape(RET, REC, 2 * HD)
    full_block = fetched.shape[1]
    positions = rec_index[0]
    onehot = positions[:, :, None] == jnp.arange(full_block, dtype=jnp.int32)[None, None, :]
    placed = jnp.einsum(
        "kib,kic->kbc", onehot.astype(jnp.bfloat16), own_rows, preferred_element_type=jnp.float32
    ).astype(jnp.bfloat16)
    replaced_at = jnp.any(onehot, axis=1)
    blocks = jnp.where(replaced_at[:, :, None], placed, fetched)
    own_self = own_head(self_kv[0], KVH, HD, my_head)
    return attention(queries[0], blocks, own_self)[None]


def solution(mesh):
    dev = DEV
    groups = mesh.shape["cache"]
    view = Mesh(mesh.devices.reshape((groups,) + (2,) * len(DEV)), ("cache",) + DEV)
    placed = (
        P("cache", None, dev),
        P("cache", dev, None),
        P("cache", None, None),
        P("cache", None, dev),
        P(dev),
        P(dev, None),
        P(),
        P(),
        P("cache", None, None),
    )
    return jax.shard_map(
        shards, mesh=view, in_specs=placed, out_specs=P("cache", None, dev), check_vma=False
    )
```

```python
import functools
import math

import jax
import jax.numpy as jnp
from jax import lax
from jax.experimental import pallas as pl
from jax.experimental.pallas import tpu as pltpu
from jax.sharding import Mesh, PartitionSpec as P

D = 8192
QH = 64
KVH = 8
HD = 128
RET = 16
CAP = 4
REC = 32
DOC_GRP = 32
DEV = ("xh", "xl", "zh", "zq1", "zq0")


eps_norm = 1e-05
tile_rows = 512


def own_head(wide_rows, head_count, head_size, chosen):
    shaped = wide_rows.reshape(wide_rows.shape[:-1] + (2, head_count, head_size))
    taken = lax.dynamic_index_in_dim(shaped, chosen, shaped.ndim - 2, keepdims=False)
    return taken.reshape(wide_rows.shape[:-1] + (2 * head_size,))


def pick_heads(wide_rows, head_count, head_size, chosen):
    shaped = wide_rows.reshape(wide_rows.shape[:-1] + (2, head_count, head_size))
    taken = jnp.take(shaped, chosen, axis=shaped.ndim - 2)
    moved = jnp.moveaxis(taken, shaped.ndim - 2, 0)
    return moved.reshape(moved.shape[:-2] + (2 * head_size,))


def attn_kernel(q_ref, kd_ref, vd_ref, ks_ref, vs_ref, o_ref, m_sc, l_sc, acc_sc, *, n_doc, n_self, blk_self, inv_root, heads):
    phase = pl.program_id(0)
    j = pl.program_id(1)

    @pl.when((phase == 0) & (j == 0))
    def _():
        m_sc[...] = jnp.full(m_sc.shape, -jnp.inf, jnp.float32)
        l_sc[...] = jnp.zeros(l_sc.shape, jnp.float32)
        acc_sc[...] = jnp.zeros(acc_sc.shape, jnp.float32)

    def scores(h, k_ref, first_key):
        q = q_ref[:, h * HD:(h + 1) * HD]
        s = lax.dot_general(q, k_ref[...], (((1,), (1,)), ((), ())), preferred_element_type=jnp.float32) * inv_root
        if first_key is None:
            return s
        t = lax.broadcasted_iota(jnp.int32, s.shape, 0)
        u = lax.broadcasted_iota(jnp.int32, s.shape, 1) + first_key
        return jnp.where(u <= t, s, -jnp.inf)

    def step(k_ref, v_ref, first_key):
        @pl.when(phase == 0)
        def _():
            for h in range(heads):
                s = scores(h, k_ref, first_key)
                m_sc[h] = jnp.maximum(m_sc[h], jnp.max(s, axis=1, keepdims=True))

        @pl.when(phase == 1)
        def _():
            for h in range(heads):
                s = scores(h, k_ref, first_key)
                e = jnp.exp(s - m_sc[h][:, :1])
                l_sc[h] = l_sc[h] + jnp.sum(e, axis=1, keepdims=True)
                acc_sc[h] = acc_sc[h] + jnp.dot(e.astype(jnp.bfloat16), v_ref[...], preferred_element_type=jnp.float32)

    @pl.when(j < n_doc)
    def _():
        step(kd_ref, vd_ref, None)

    for b in range(n_self):
        @pl.when(j == n_doc + b)
        def _(b=b):
            step(ks_ref, vs_ref, b * blk_self)

    @pl.when((phase == 1) & (j == pl.num_programs(1) - 1))
    def _():
        for h in range(heads):
            o_ref[:, h * HD:(h + 1) * HD] = (acc_sc[h] / l_sc[h][:, :1]).astype(o_ref.dtype)


def attention(q2d, blocks, own_self, bk=2048):
    T, width = q2d.shape
    heads = width // HD
    flat = blocks.reshape(-1, blocks.shape[-1])
    n_doc = flat.shape[0] // bk
    bs = min(bk, T)
    n_self = T // bs
    kern = functools.partial(attn_kernel, n_doc=n_doc, n_self=n_self, blk_self=bs, inv_root=1.0 / math.sqrt(HD), heads=heads)
    doc_at = lambda j: jnp.minimum(j, n_doc - 1)
    self_at = lambda j: jnp.maximum(j - n_doc, 0)
    return pl.pallas_call(
        kern,
        grid=(2, n_doc + n_self),
        in_specs=[
            pl.BlockSpec((T, width), lambda p, j: (0, 0)),
            pl.BlockSpec((bk, HD), lambda p, j: (doc_at(j), 0)),
            pl.BlockSpec((bk, HD), lambda p, j: (doc_at(j), 1)),
            pl.BlockSpec((bs, HD), lambda p, j: (self_at(j), 0)),
            pl.BlockSpec((bs, HD), lambda p, j: (self_at(j), 1)),
        ],
        out_specs=pl.BlockSpec((T, width), lambda p, j: (0, 0)),
        out_shape=jax.ShapeDtypeStruct((T, width), q2d.dtype),
        scratch_shapes=[pltpu.VMEM((heads, T, HD), jnp.float32)] * 3,
    )(q2d, flat, flat, own_self, own_self)


def pair_sum(value, axis):
    size = lax.axis_size(axis)
    step = 1
    while step < size:
        value = value + lax.ppermute(value, axis, [(i, i ^ step) for i in range(size)])
        step *= 2
    return value


def halve_sum(value, axis, dim=0):
    size = lax.axis_size(axis)
    me = lax.axis_index(axis)
    step = 1
    while step < size:
        bit = (me // step) % 2
        shape = value.shape
        halves = value.reshape(shape[:dim] + (2, shape[dim] // 2) + shape[dim + 1 :])
        keep = lax.dynamic_index_in_dim(halves, bit, dim, keepdims=False)
        send = lax.dynamic_index_in_dim(halves, 1 - bit, dim, keepdims=False)
        value = keep + lax.ppermute(send, axis, [(i, i ^ step) for i in range(size)])
        step *= 2
    return value


def double_gather(value, axis):
    size = lax.axis_size(axis)
    me = lax.axis_index(axis)
    step = size // 2
    while step >= 1:
        bit = (me // step) % 2
        other = lax.ppermute(value, axis, [(i, i ^ step) for i in range(size)])
        value = jnp.where(
            bit == 0, jnp.concatenate([value, other], axis=0), jnp.concatenate([other, value], axis=0)
        )
        step //= 2
    return value


def shards(queries, store_kv, self_kv, rec_states, norm_gain, w_kv, retrieval, doc_home, rec_index):
    groups = lax.axis_size("cache")
    members = lax.axis_size(DEV)
    my_group = lax.axis_index("cache")
    my_member = lax.axis_index(DEV)
    per_device = QH // members
    ratio_heads = QH // KVH
    my_head = my_member * per_device // ratio_heads
    shard_rows = store_kv.shape[1]
    kv_width = store_kv.shape[2]
    inv_root = 1.0 / math.sqrt(HD)
    stored_at = jnp.take(doc_home, retrieval, axis=0)
    source = stored_at // DOC_GRP
    local_row = stored_at % DOC_GRP
    before = jnp.arange(RET)[None, :] < jnp.arange(RET)[:, None]
    same_home = source[:, :, None] == source[:, None, :]
    rank_within = jnp.sum((same_home & before[None, :, :]).astype(jnp.int32), axis=2)
    places = jnp.arange(CAP, dtype=jnp.int32)
    matching = (source[:, None, :] == my_group) & (rank_within[:, None, :] == places[None, :, None])
    pick_row = jnp.sum(jnp.where(matching, local_row[:, None, :], 0), axis=2)
    filled = jnp.any(matching, axis=2)
    outgoing = jnp.take(store_kv, pick_row.reshape(-1), axis=0).reshape(
        groups, CAP, shard_rows, kv_width
    )
    outgoing = jnp.where(filled[:, :, None, None], outgoing, jnp.zeros((), store_kv.dtype))
    my_source = lax.dynamic_index_in_dim(source, my_group, 0, keepdims=False)
    my_rank = lax.dynamic_index_in_dim(rank_within, my_group, 0, keepdims=False)
    slot_place = my_source * CAP + my_rank
    dest_heads = jnp.arange(members, dtype=jnp.int32) * per_device // ratio_heads
    arrived = lax.all_to_all(outgoing, "cache", split_axis=0, concat_axis=0, tiled=True)
    compact = jnp.take(arrived.reshape(groups * CAP, shard_rows, kv_width), slot_place, axis=0)
    spread = pick_heads(compact, KVH, HD, dest_heads)
    fetched = lax.all_to_all(spread, DEV, split_axis=0, concat_axis=2, tiled=True)[0]
    states = rec_states[0].astype(jnp.float32)
    rows_rec = states.shape[0]
    partial_sq = jnp.sum(states * states, axis=1)
    sq_rows = jnp.broadcast_to(partial_sq[None, :], (members, rows_rec))
    total_sq = jnp.sum(lax.all_to_all(sq_rows, DEV, split_axis=0, concat_axis=0, tiled=True), axis=0)
    inv_rms = lax.rsqrt(total_sq / D + eps_norm)
    normed = (states * norm_gain.astype(jnp.float32)[None, :] * inv_rms[:, None]).astype(jnp.bfloat16)
    w_rows = w_kv.shape[0]
    w_order = jnp.transpose(w_kv.reshape(w_rows, 2, 2, 2, 2, HD), (0, 3, 1, 2, 4, 5)).reshape(w_rows, -1)
    partial_kv = jnp.dot(normed, w_order, preferred_element_type=jnp.float32)
    row_part = halve_sum(partial_kv, "zq0")
    half_rows = row_part.shape[0]
    head_part = halve_sum(row_part.reshape(half_rows, 2, -1), "xl", 1)
    part_rows = half_rows // 2
    by_dest = jnp.transpose(head_part.reshape(2, part_rows, 2, 2, 2, HD), (3, 4, 0, 1, 2, 5))
    by_dest = by_dest.reshape(KVH, part_rows, 2, HD)
    head_parts = lax.all_to_all(by_dest, ("xh", "zh", "zq1"), split_axis=0, concat_axis=0, tiled=True)
    head_rows = jnp.sum(head_parts, axis=0).reshape(part_rows, 2 * HD).astype(jnp.bfloat16)
    redone = double_gather(head_rows, ("zq1", "zq0"))
    own_rows = redone.reshape(RET, REC, 2 * HD)
    full_block = fetched.shape[1]
    positions = rec_index[0]
    onehot = positions[:, :, None] == jnp.arange(full_block, dtype=jnp.int32)[None, None, :]
    placed = jnp.einsum(
        "kib,kic->kbc", onehot.astype(jnp.bfloat16), own_rows, preferred_element_type=jnp.float32
    ).astype(jnp.bfloat16)
    replaced_at = jnp.any(onehot, axis=1)
    blocks = jnp.where(replaced_at[:, :, None], placed, fetched)
    own_self = own_head(self_kv[0], KVH, HD, my_head)
    return attention(queries[0], blocks, own_self)[None]


def solution(mesh):
    dev = DEV
    groups = mesh.shape["cache"]
    view = Mesh(mesh.devices.reshape((groups,) + (2,) * len(DEV)), ("cache",) + DEV)
    placed = (
        P("cache", None, dev),
        P("cache", dev, None),
        P("cache", None, None),
        P("cache", None, dev),
        P(dev),
        P(dev, None),
        P(),
        P(),
        P("cache", None, None),
    )
    return jax.shard_map(
        shards, mesh=view, in_specs=placed, out_specs=P("cache", None, dev), check_vma=False
    )
```

```python
import functools
import math

import jax
import jax.numpy as jnp
from jax import lax
from jax.experimental import pallas as pl
from jax.experimental.pallas import tpu as pltpu
from jax.sharding import Mesh, PartitionSpec as P

D = 8192
QH = 64
KVH = 8
HD = 128
RET = 16
CAP = 4
REC = 32
DOC_GRP = 32
DEV = ("xh", "xl", "zh", "zq1", "zq0")


eps_norm = 1e-05
tile_rows = 512


def own_head(wide_rows, head_count, head_size, chosen):
    shaped = wide_rows.reshape(wide_rows.shape[:-1] + (2, head_count, head_size))
    taken = lax.dynamic_index_in_dim(shaped, chosen, shaped.ndim - 2, keepdims=False)
    return taken.reshape(wide_rows.shape[:-1] + (2 * head_size,))


def pick_heads(wide_rows, head_count, head_size, chosen):
    shaped = wide_rows.reshape(wide_rows.shape[:-1] + (2, head_count, head_size))
    taken = jnp.take(shaped, chosen, axis=shaped.ndim - 2)
    moved = jnp.moveaxis(taken, shaped.ndim - 2, 0)
    return moved.reshape(moved.shape[:-2] + (2 * head_size,))


def attn_kernel(q_ref, kd_ref, vd_ref, ks_ref, vs_ref, o_ref, m_sc, l_sc, acc_sc, *, n_doc, n_self, blk_self, inv_root, heads):
    phase = pl.program_id(0)
    j = pl.program_id(1)

    @pl.when((phase == 0) & (j == 0))
    def _():
        m_sc[...] = jnp.full(m_sc.shape, -jnp.inf, jnp.float32)
        l_sc[...] = jnp.zeros(l_sc.shape, jnp.float32)
        acc_sc[...] = jnp.zeros(acc_sc.shape, jnp.float32)

    def scores(h, k_ref, first_key):
        q = q_ref[:, h * HD:(h + 1) * HD]
        s = lax.dot_general(q, k_ref[...], (((1,), (1,)), ((), ())), preferred_element_type=jnp.float32) * inv_root
        if first_key is None:
            return s
        t = lax.broadcasted_iota(jnp.int32, s.shape, 0)
        u = lax.broadcasted_iota(jnp.int32, s.shape, 1) + first_key
        return jnp.where(u <= t, s, -jnp.inf)

    def step(k_ref, v_ref, first_key):
        @pl.when(phase == 0)
        def _():
            for h in range(heads):
                s = scores(h, k_ref, first_key)
                m_sc[h] = jnp.maximum(m_sc[h], jnp.max(s, axis=1, keepdims=True))

        @pl.when(phase == 1)
        def _():
            for h in range(heads):
                s = scores(h, k_ref, first_key)
                e = jnp.exp(s - m_sc[h][:, :1])
                l_sc[h] = l_sc[h] + jnp.sum(e, axis=1, keepdims=True)
                acc_sc[h] = acc_sc[h] + jnp.dot(e.astype(jnp.bfloat16), v_ref[...], preferred_element_type=jnp.float32)

    @pl.when(j < n_doc)
    def _():
        step(kd_ref, vd_ref, None)

    for b in range(n_self):
        @pl.when(j == n_doc + b)
        def _(b=b):
            step(ks_ref, vs_ref, b * blk_self)

    @pl.when((phase == 1) & (j == pl.num_programs(1) - 1))
    def _():
        for h in range(heads):
            o_ref[:, h * HD:(h + 1) * HD] = (acc_sc[h] / l_sc[h][:, :1]).astype(o_ref.dtype)


def attention(q2d, blocks, own_self, bk=2048):
    T, width = q2d.shape
    heads = width // HD
    flat = blocks.reshape(-1, blocks.shape[-1])
    n_doc = flat.shape[0] // bk
    bs = min(bk, T)
    n_self = T // bs
    kern = functools.partial(attn_kernel, n_doc=n_doc, n_self=n_self, blk_self=bs, inv_root=1.0 / math.sqrt(HD), heads=heads)
    doc_at = lambda j: jnp.minimum(j, n_doc - 1)
    self_at = lambda j: jnp.maximum(j - n_doc, 0)
    return pl.pallas_call(
        kern,
        grid=(2, n_doc + n_self),
        in_specs=[
            pl.BlockSpec((T, width), lambda p, j: (0, 0)),
            pl.BlockSpec((bk, HD), lambda p, j: (doc_at(j), 0)),
            pl.BlockSpec((bk, HD), lambda p, j: (doc_at(j), 1)),
            pl.BlockSpec((bs, HD), lambda p, j: (self_at(j), 0)),
            pl.BlockSpec((bs, HD), lambda p, j: (self_at(j), 1)),
        ],
        out_specs=pl.BlockSpec((T, width), lambda p, j: (0, 0)),
        out_shape=jax.ShapeDtypeStruct((T, width), q2d.dtype),
        scratch_shapes=[pltpu.VMEM((heads, T, HD), jnp.float32)] * 3,
    )(q2d, flat, flat, own_self, own_self)


def pair_sum(value, axis):
    size = lax.axis_size(axis)
    step = 1
    while step < size:
        value = value + lax.ppermute(value, axis, [(i, i ^ step) for i in range(size)])
        step *= 2
    return value


def halve_sum(value, axis, dim=0):
    size = lax.axis_size(axis)
    me = lax.axis_index(axis)
    step = 1
    while step < size:
        bit = (me // step) % 2
        shape = value.shape
        halves = value.reshape(shape[:dim] + (2, shape[dim] // 2) + shape[dim + 1 :])
        keep = lax.dynamic_index_in_dim(halves, bit, dim, keepdims=False)
        send = lax.dynamic_index_in_dim(halves, 1 - bit, dim, keepdims=False)
        value = keep + lax.ppermute(send, axis, [(i, i ^ step) for i in range(size)])
        step *= 2
    return value


def double_gather(value, axis):
    size = lax.axis_size(axis)
    me = lax.axis_index(axis)
    step = size // 2
    while step >= 1:
        bit = (me // step) % 2
        other = lax.ppermute(value, axis, [(i, i ^ step) for i in range(size)])
        value = jnp.where(
            bit == 0, jnp.concatenate([value, other], axis=0), jnp.concatenate([other, value], axis=0)
        )
        step //= 2
    return value


def shards(queries, store_kv, self_kv, rec_states, norm_gain, w_kv, retrieval, doc_home, rec_index):
    groups = lax.axis_size("cache")
    members = lax.axis_size(DEV)
    my_group = lax.axis_index("cache")
    my_member = lax.axis_index(DEV)
    per_device = QH // members
    ratio_heads = QH // KVH
    my_head = my_member * per_device // ratio_heads
    shard_rows = store_kv.shape[1]
    kv_width = store_kv.shape[2]
    inv_root = 1.0 / math.sqrt(HD)
    stored_at = jnp.take(doc_home, retrieval, axis=0)
    source = stored_at // DOC_GRP
    local_row = stored_at % DOC_GRP
    before = jnp.arange(RET)[None, :] < jnp.arange(RET)[:, None]
    same_home = source[:, :, None] == source[:, None, :]
    rank_within = jnp.sum((same_home & before[None, :, :]).astype(jnp.int32), axis=2)
    places = jnp.arange(CAP, dtype=jnp.int32)
    matching = (source[:, None, :] == my_group) & (rank_within[:, None, :] == places[None, :, None])
    pick_row = jnp.sum(jnp.where(matching, local_row[:, None, :], 0), axis=2)
    filled = jnp.any(matching, axis=2)
    outgoing = jnp.take(store_kv, pick_row.reshape(-1), axis=0).reshape(
        groups, CAP, shard_rows, kv_width
    )
    outgoing = jnp.where(filled[:, :, None, None], outgoing, jnp.zeros((), store_kv.dtype))
    my_source = lax.dynamic_index_in_dim(source, my_group, 0, keepdims=False)
    my_rank = lax.dynamic_index_in_dim(rank_within, my_group, 0, keepdims=False)
    slot_place = my_source * CAP + my_rank
    dest_heads = jnp.arange(members, dtype=jnp.int32) * per_device // ratio_heads
    arrived = lax.all_to_all(outgoing, "cache", split_axis=0, concat_axis=0, tiled=True)
    compact = jnp.take(arrived.reshape(groups * CAP, shard_rows, kv_width), slot_place, axis=0)
    spread = pick_heads(compact, KVH, HD, dest_heads)
    fetched = lax.all_to_all(spread, DEV, split_axis=0, concat_axis=2, tiled=True)[0]
    states = rec_states[0].astype(jnp.float32)
    rows_rec = states.shape[0]
    partial_sq = jnp.sum(states * states, axis=1)
    sq_rows = jnp.broadcast_to(partial_sq[None, :], (members, rows_rec))
    total_sq = jnp.sum(lax.all_to_all(sq_rows, DEV, split_axis=0, concat_axis=0, tiled=True), axis=0)
    inv_rms = lax.rsqrt(total_sq / D + eps_norm)
    normed = (states * norm_gain.astype(jnp.float32)[None, :] * inv_rms[:, None]).astype(jnp.bfloat16)
    partial_kv = jnp.dot(normed, w_kv, preferred_element_type=jnp.float32)
    head_first = halve_sum(partial_kv.reshape(rows_rec, 2, 2, 2, 2, HD), "xl", 3)
    head_part = halve_sum(head_first, "zq0")
    part_rows = head_part.shape[0] // 2
    by_dest = jnp.transpose(head_part.reshape(2, part_rows, 2, 2, 2, HD), (3, 4, 0, 1, 2, 5))
    by_dest = by_dest.reshape(KVH, part_rows, 2, HD)
    head_parts = lax.all_to_all(by_dest, ("xh", "zh", "zq1"), split_axis=0, concat_axis=0, tiled=True)
    head_rows = jnp.sum(head_parts, axis=0).reshape(part_rows, 2 * HD).astype(jnp.bfloat16)
    redone = double_gather(head_rows, ("zq1", "zq0"))
    own_rows = redone.reshape(RET, REC, 2 * HD)
    full_block = fetched.shape[1]
    positions = rec_index[0]
    onehot = positions[:, :, None] == jnp.arange(full_block, dtype=jnp.int32)[None, None, :]
    placed = jnp.einsum(
        "kib,kic->kbc", onehot.astype(jnp.bfloat16), own_rows, preferred_element_type=jnp.float32
    ).astype(jnp.bfloat16)
    replaced_at = jnp.any(onehot, axis=1)
    blocks = jnp.where(replaced_at[:, :, None], placed, fetched)
    own_self = own_head(self_kv[0], KVH, HD, my_head)
    return attention(queries[0], blocks, own_self)[None]


def solution(mesh):
    dev = DEV
    groups = mesh.shape["cache"]
    view = Mesh(mesh.devices.reshape((groups,) + (2,) * len(DEV)), ("cache",) + DEV)
    placed = (
        P("cache", None, dev),
        P("cache", dev, None),
        P("cache", None, None),
        P("cache", None, dev),
        P(dev),
        P(dev, None),
        P(),
        P(),
        P("cache", None, None),
    )
    return jax.shard_map(
        shards, mesh=view, in_specs=placed, out_specs=P("cache", None, dev), check_vma=False
    )
```

```python
import functools
import math

import jax
import jax.numpy as jnp
from jax import lax
from jax.experimental import pallas as pl
from jax.experimental.pallas import tpu as pltpu
from jax.sharding import Mesh, PartitionSpec as P

D = 8192
QH = 64
KVH = 8
HD = 128
RET = 16
CAP = 4
REC = 32
DOC_GRP = 32
DEV = ("xh", "xl", "zh", "zq1", "zq0")


eps_norm = 1e-05
tile_rows = 512


def own_head(wide_rows, head_count, head_size, chosen):
    shaped = wide_rows.reshape(wide_rows.shape[:-1] + (2, head_count, head_size))
    taken = lax.dynamic_index_in_dim(shaped, chosen, shaped.ndim - 2, keepdims=False)
    return taken.reshape(wide_rows.shape[:-1] + (2 * head_size,))


def pick_heads(wide_rows, head_count, head_size, chosen):
    shaped = wide_rows.reshape(wide_rows.shape[:-1] + (2, head_count, head_size))
    taken = jnp.take(shaped, chosen, axis=shaped.ndim - 2)
    moved = jnp.moveaxis(taken, shaped.ndim - 2, 0)
    return moved.reshape(moved.shape[:-2] + (2 * head_size,))


def attn_kernel(q_ref, kd_ref, vd_ref, ks_ref, vs_ref, o_ref, m_sc, l_sc, acc_sc, *, n_doc, n_self, blk_self, inv_root, heads):
    phase = pl.program_id(0)
    j = pl.program_id(1)

    @pl.when((phase == 0) & (j == 0))
    def _():
        m_sc[...] = jnp.full(m_sc.shape, -jnp.inf, jnp.float32)
        l_sc[...] = jnp.zeros(l_sc.shape, jnp.float32)
        acc_sc[...] = jnp.zeros(acc_sc.shape, jnp.float32)

    def scores(h, k_ref, first_key):
        q = q_ref[:, h * HD:(h + 1) * HD]
        s = lax.dot_general(q, k_ref[...], (((1,), (1,)), ((), ())), preferred_element_type=jnp.float32) * inv_root
        if first_key is None:
            return s
        t = lax.broadcasted_iota(jnp.int32, s.shape, 0)
        u = lax.broadcasted_iota(jnp.int32, s.shape, 1) + first_key
        return jnp.where(u <= t, s, -jnp.inf)

    def step(k_ref, v_ref, first_key):
        @pl.when(phase == 0)
        def _():
            for h in range(heads):
                s = scores(h, k_ref, first_key)
                m_sc[h] = jnp.maximum(m_sc[h], jnp.max(s, axis=1, keepdims=True))

        @pl.when(phase == 1)
        def _():
            for h in range(heads):
                s = scores(h, k_ref, first_key)
                e = jnp.exp(s - m_sc[h][:, :1])
                l_sc[h] = l_sc[h] + jnp.sum(e, axis=1, keepdims=True)
                acc_sc[h] = acc_sc[h] + jnp.dot(e.astype(jnp.bfloat16), v_ref[...], preferred_element_type=jnp.float32)

    @pl.when(j < n_doc)
    def _():
        step(kd_ref, vd_ref, None)

    for b in range(n_self):
        @pl.when(j == n_doc + b)
        def _(b=b):
            step(ks_ref, vs_ref, b * blk_self)

    @pl.when((phase == 1) & (j == pl.num_programs(1) - 1))
    def _():
        for h in range(heads):
            o_ref[:, h * HD:(h + 1) * HD] = (acc_sc[h] / l_sc[h][:, :1]).astype(o_ref.dtype)


def attention(q2d, blocks, own_self, bk=2048):
    T, width = q2d.shape
    heads = width // HD
    flat = blocks.reshape(-1, blocks.shape[-1])
    n_doc = flat.shape[0] // bk
    bs = min(bk, T)
    n_self = T // bs
    kern = functools.partial(attn_kernel, n_doc=n_doc, n_self=n_self, blk_self=bs, inv_root=1.0 / math.sqrt(HD), heads=heads)
    doc_at = lambda j: jnp.minimum(j, n_doc - 1)
    self_at = lambda j: jnp.maximum(j - n_doc, 0)
    return pl.pallas_call(
        kern,
        grid=(2, n_doc + n_self),
        in_specs=[
            pl.BlockSpec((T, width), lambda p, j: (0, 0)),
            pl.BlockSpec((bk, HD), lambda p, j: (doc_at(j), 0)),
            pl.BlockSpec((bk, HD), lambda p, j: (doc_at(j), 1)),
            pl.BlockSpec((bs, HD), lambda p, j: (self_at(j), 0)),
            pl.BlockSpec((bs, HD), lambda p, j: (self_at(j), 1)),
        ],
        out_specs=pl.BlockSpec((T, width), lambda p, j: (0, 0)),
        out_shape=jax.ShapeDtypeStruct((T, width), q2d.dtype),
        scratch_shapes=[pltpu.VMEM((heads, T, HD), jnp.float32)] * 3,
    )(q2d, flat, flat, own_self, own_self)


def pair_sum(value, axis):
    size = lax.axis_size(axis)
    step = 1
    while step < size:
        value = value + lax.ppermute(value, axis, [(i, i ^ step) for i in range(size)])
        step *= 2
    return value


def halve_sum(value, axis, dim=0):
    size = lax.axis_size(axis)
    me = lax.axis_index(axis)
    step = 1
    while step < size:
        bit = (me // step) % 2
        shape = value.shape
        halves = value.reshape(shape[:dim] + (2, shape[dim] // 2) + shape[dim + 1 :])
        keep = lax.dynamic_index_in_dim(halves, bit, dim, keepdims=False)
        send = lax.dynamic_index_in_dim(halves, 1 - bit, dim, keepdims=False)
        value = keep + lax.ppermute(send, axis, [(i, i ^ step) for i in range(size)])
        step *= 2
    return value


def double_gather(value, axis):
    size = lax.axis_size(axis)
    me = lax.axis_index(axis)
    step = size // 2
    while step >= 1:
        bit = (me // step) % 2
        other = lax.ppermute(value, axis, [(i, i ^ step) for i in range(size)])
        value = jnp.where(
            bit == 0, jnp.concatenate([value, other], axis=0), jnp.concatenate([other, value], axis=0)
        )
        step //= 2
    return value


def shards(queries, store_kv, self_kv, rec_states, norm_gain, w_kv, retrieval, doc_home, rec_index):
    groups = lax.axis_size("cache")
    members = lax.axis_size(DEV)
    my_group = lax.axis_index("cache")
    my_member = lax.axis_index(DEV)
    per_device = QH // members
    ratio_heads = QH // KVH
    my_head = my_member * per_device // ratio_heads
    shard_rows = store_kv.shape[1]
    kv_width = store_kv.shape[2]
    inv_root = 1.0 / math.sqrt(HD)
    stored_at = jnp.take(doc_home, retrieval, axis=0)
    source = stored_at // DOC_GRP
    local_row = stored_at % DOC_GRP
    before = jnp.arange(RET)[None, :] < jnp.arange(RET)[:, None]
    same_home = source[:, :, None] == source[:, None, :]
    rank_within = jnp.sum((same_home & before[None, :, :]).astype(jnp.int32), axis=2)
    places = jnp.arange(CAP, dtype=jnp.int32)
    matching = (source[:, None, :] == my_group) & (rank_within[:, None, :] == places[None, :, None])
    pick_row = jnp.sum(jnp.where(matching, local_row[:, None, :], 0), axis=2)
    filled = jnp.any(matching, axis=2)
    outgoing = jnp.take(store_kv, pick_row.reshape(-1), axis=0).reshape(
        groups, CAP, shard_rows, kv_width
    )
    outgoing = jnp.where(filled[:, :, None, None], outgoing, jnp.zeros((), store_kv.dtype))
    my_source = lax.dynamic_index_in_dim(source, my_group, 0, keepdims=False)
    my_rank = lax.dynamic_index_in_dim(rank_within, my_group, 0, keepdims=False)
    slot_place = my_source * CAP + my_rank
    dest_heads = jnp.arange(members, dtype=jnp.int32) * per_device // ratio_heads
    arrived = lax.all_to_all(outgoing, "cache", split_axis=0, concat_axis=0, tiled=True)
    compact = jnp.take(arrived.reshape(groups * CAP, shard_rows, kv_width), slot_place, axis=0)
    spread = pick_heads(compact, KVH, HD, dest_heads)
    fetched = lax.all_to_all(spread, DEV, split_axis=0, concat_axis=2, tiled=True)[0]
    states = rec_states[0].astype(jnp.float32)
    rows_rec = states.shape[0]
    partial_sq = jnp.sum(states * states, axis=1)
    sq_rows = jnp.broadcast_to(partial_sq[None, :], (members, rows_rec))
    total_sq = jnp.sum(lax.all_to_all(sq_rows, DEV, split_axis=0, concat_axis=0, tiled=True), axis=0)
    inv_rms = lax.rsqrt(total_sq / D + eps_norm)
    normed = (states * norm_gain.astype(jnp.float32)[None, :] * inv_rms[:, None]).astype(jnp.bfloat16)
    partial_kv = jnp.dot(normed, w_kv, preferred_element_type=jnp.float32)
    head_first = halve_sum(partial_kv.reshape(rows_rec, 2, 2, 2, 2, HD), "xl", 3)
    quarter = halve_sum(halve_sum(head_first, "zq0"), "zq1")
    part_rows = quarter.shape[0]
    by_dest = jnp.transpose(quarter.reshape(part_rows, 2, 2, 2, HD), (2, 3, 0, 1, 4))
    by_dest = by_dest.reshape(-1, part_rows, 2, HD)
    head_parts = lax.all_to_all(by_dest, ("xh", "zh"), split_axis=0, concat_axis=0, tiled=True)
    head_rows = jnp.sum(head_parts, axis=0).reshape(part_rows, 2 * HD).astype(jnp.bfloat16)
    redone = double_gather(head_rows, ("zq1", "zq0"))
    own_rows = redone.reshape(RET, REC, 2 * HD)
    full_block = fetched.shape[1]
    positions = rec_index[0]
    onehot = positions[:, :, None] == jnp.arange(full_block, dtype=jnp.int32)[None, None, :]
    placed = jnp.einsum(
        "kib,kic->kbc", onehot.astype(jnp.bfloat16), own_rows, preferred_element_type=jnp.float32
    ).astype(jnp.bfloat16)
    replaced_at = jnp.any(onehot, axis=1)
    blocks = jnp.where(replaced_at[:, :, None], placed, fetched)
    own_self = own_head(self_kv[0], KVH, HD, my_head)
    return attention(queries[0], blocks, own_self)[None]


def solution(mesh):
    dev = DEV
    groups = mesh.shape["cache"]
    view = Mesh(mesh.devices.reshape((groups,) + (2,) * len(DEV)), ("cache",) + DEV)
    placed = (
        P("cache", None, dev),
        P("cache", dev, None),
        P("cache", None, None),
        P("cache", None, dev),
        P(dev),
        P(dev, None),
        P(),
        P(),
        P("cache", None, None),
    )
    return jax.shard_map(
        shards, mesh=view, in_specs=placed, out_specs=P("cache", None, dev), check_vma=False
    )
```
